32 devices in a mesh: gx: 4 (over y, x), gy: 8 (over z, core).
Axes of the slice: x: 2, y: 2, z: 4, core: 2. Of those that a mesh axis runs over, the one named last changes fastest.
Arguments:
- stream_in: bfloat16 [64, 1536], P(None, 'gx'), may hold values from -60 to 60
- attention_gain: float32 [2, 1536], P(None, 'gx'), may hold values from 0.5 to 1.5
- feedforward_gain: float32 [2, 1536], P(None, 'gx'), may hold values from 0.5 to 1.5
- final_gain: float32 [1536], P('gx'), may hold values from 0.5 to 1.5
- qkv_weight: bfloat16 [2, 1536, 3072], P(None, 'gx', 'gy'), may hold values from -0.15625 to 0.15625
- forget_weight: bfloat16 [2, 1536, 16], P(None, 'gx', 'gy'), may hold values from -0.15625 to 0.15625
- forget_bias: float32 [2, 16], P(None, 'gy'), may hold values from -2 to 3
- out_weight: bfloat16 [2, 1024, 1536], P(None, 'gy', 'gx'), may hold values from -0.1875 to 0.1875
- gate_weight: bfloat16 [2, 1536, 4096], P(None, 'gx', 'gy'), may hold values from -0.15625 to 0.15625
- up_weight: bfloat16 [2, 1536, 4096], P(None, 'gx', 'gy'), may hold values from -0.15625 to 0.15625
- down_weight: bfloat16 [2, 4096, 1536], P(None, 'gy', 'gx'), may hold values from -0.09375 to 0.09375
- head_weight: bfloat16 [1536, 49152], P('gx', 'gy'), may hold values from -0.15625 to 0.15625
- kv_cache: bfloat16 [2, 512, 128, 16, 128], P(None, 'gx', None, 'gy'), may hold values from -102 to 102
- decay_cache: float32 [2, 512, 16, 128], P(None, 'gx', 'gy'), may hold values from -66 to 0
- lengths: int32 [64], replicated, may hold values from 1 to 32768, as said below
- page_table: int32 [64, 256], replicated, may hold values from -1 to 511, as said below
Outputs:
- final_hidden: bfloat16 [64, 1536], P(None, 'gx')
- row_norms: float32 [64], replicated
- top_logits: float32 [64], replicated
The draws below stay inside these ranges and needn't reach their ends.
Inputs may be any that keep to these rules, and one draw needn't show every extreme that they name: `lengths`: every request has at least one cached token and one request has exactly 32768. `page_table`: row r names the slots of its first ceil(lengths[r] / 128) pages and holds -1 after them; no slot is named twice; slot s lies in block s // 128 of gx.
All inputs are finite; a program needn't handle non-finite values.
Results may differ from the reference program's by a relative error of at most 0.01.
The reference program's roundings to bfloat16 on the way (of `normed`, `queries`, `rounded`, `attended` and `hidden`) count: a program that leaves them out, or rounds other values in their place, can miss the bound.
Values may be sent and summed in bfloat16 or wider, within the bound.
No kernel may reach another device: no remote copies, remote signals or barrier semaphores. Data moves between devices by JAX's collectives and lax.ppermute only.
A program may use at most 128 MiB of HBM per device.

```python
import jax
import jax.numpy as jnp
from jax import lax

D = 1536
FF = 4096
PORTION_FOCI = 16
HEAD = 64
VOCAB = 49152
DEPTH_NUMBER = 2
SHEET_ENTRIES = 128
REQUESTS = 64
SHEETS_OVERALL = 512
MAX_PAGES = 256


def request_layout(key):
    folded = jax.random.fold_in(key, 5)
    key_order, key_level, key_extra, key_fill, key_slot = jax.random.split(folded, 5)
    levels_top = MAX_PAGES.bit_length() - 1
    request_order = jax.random.permutation(key_order, REQUESTS)
    levels = jax.random.randint(key_level, (REQUESTS,), 0, levels_top + 1)
    extra_pages = jax.random.randint(key_extra, (REQUESTS,), 0, jnp.left_shift(1, levels))
    extra_pages = jnp.minimum(extra_pages, MAX_PAGES - 1)
    rank_ids = jnp.arange(REQUESTS, dtype=jnp.int32)
    extra_pages = jnp.where(rank_ids == 0, MAX_PAGES - 1, extra_pages)
    spare_pages = SHEETS_OVERALL - REQUESTS
    before = jnp.cumsum(extra_pages) - extra_pages
    granted = jnp.clip(spare_pages - before, 0, extra_pages)
    counts = 1 + granted
    last_fill = jax.random.randint(key_fill, (REQUESTS,), 1, SHEET_ENTRIES + 1)
    last_fill = jnp.where(rank_ids == 0, SHEET_ENTRIES, last_fill)
    sizes_ranked = (counts - 1) * SHEET_ENTRIES + last_fill
    first_slot = jnp.cumsum(counts) - counts
    free_slots = jax.random.permutation(key_slot, SHEETS_OVERALL)
    page_ids = jnp.arange(MAX_PAGES, dtype=jnp.int32)
    within = page_ids[None, :] < counts[:, None]
    where_slot = jnp.clip(first_slot[:, None] + page_ids[None, :], 0, SHEETS_OVERALL - 1)
    rows_ranked = jnp.where(within, free_slots[where_slot], -1)
    lengths_out = jnp.zeros((REQUESTS,), jnp.int32).at[request_order].set(sizes_ranked.astype(jnp.int32))
    page_rows = jnp.zeros((REQUESTS, MAX_PAGES), jnp.int32).at[request_order].set(rows_ranked.astype(jnp.int32))
    return (lengths_out, page_rows)


def draw_lengths(key, part):
    return request_layout(key)[0]


def draw_page_table(key, part):
    return request_layout(key)[1]


def draw_stream_in(key, part):
    key_base, key_rough = jax.random.split(jax.random.fold_in(key, 29), 2)
    position = jnp.arange(D, dtype=jnp.float32) / (D - 1)
    rough = jax.random.uniform(key_rough, (1, D), jnp.float32, 0.7, 1.4)
    ramp = jnp.exp(jnp.log(0.5) + jnp.log(10.0) * position)[None, :]
    base = jnp.clip(jax.random.normal(key_base, (REQUESTS, D), jnp.float32), -6.0, 6.0)
    values = base * ramp * rough
    return values.astype(jnp.bfloat16)


def draw_kv_cache(key, part):
    key_base = jax.random.fold_in(jax.random.fold_in(key, 13), 0)
    shape = (DEPTH_NUMBER, SHEETS_OVERALL, SHEET_ENTRIES, PORTION_FOCI, 2 * HEAD)
    values = jnp.clip(jax.random.normal(key_base, shape, jnp.float32), -6.0, 6.0)
    return values.astype(jnp.bfloat16)


def draw_decay_cache(key, part):
    speed_seed, elapsed_seed, spike_seed, extent_seed = jax.random.split(jax.random.fold_in(key, 17), 4)
    low_rate, high_rate = (0.01, 1.0)
    exponents = jax.random.uniform(speed_seed, (DEPTH_NUMBER, 1, PORTION_FOCI, 1), jnp.float32, jnp.log(low_rate), jnp.log(high_rate))
    fading_speeds = jnp.exp(exponents)
    entry_elapsed = jax.random.uniform(elapsed_seed, (DEPTH_NUMBER, SHEETS_OVERALL, PORTION_FOCI, SHEET_ENTRIES), jnp.float32, 0.0, 64.0)
    spike_clusters = jax.random.uniform(spike_seed, (DEPTH_NUMBER, SHEETS_OVERALL, PORTION_FOCI, SHEET_ENTRIES), jnp.float32) < 0.05
    spike_span = jax.random.uniform(extent_seed, (DEPTH_NUMBER, SHEETS_OVERALL, PORTION_FOCI, SHEET_ENTRIES), jnp.float32, 0.2, 0.7)
    return -(fading_speeds * entry_elapsed + jnp.where(spike_clusters, spike_span, 0.0))


def block_scale(rng, dims, shards, least, top_value):
    factor_of, own = 1.0, jax.random.fold_in(rng, 6)
    for axis_at, blocks in shards:
        heights = jnp.exp(jax.random.uniform(jax.random.fold_in(own, axis_at), (blocks,), jnp.float32, least / len(shards), top_value / len(shards)))
        factor_of = factor_of * jnp.repeat(heights, dims[axis_at] // blocks).reshape([-1 if axis == axis_at else 1 for axis in range(len(dims))])
    return factor_of


def normal_values(key, extent, scale, limit, cuts=(), kind=jnp.bfloat16):
    loudness = block_scale(key, extent, cuts, -0.22, 0.18) if cuts else 1.0
    entries = jax.random.normal(key, extent, jnp.float32) * scale * loudness
    return jnp.minimum(jnp.maximum(entries, -limit), limit).astype(kind)


def setup_inputs(seed: int = 0) -> dict:
    keys = jax.random.split(jax.random.key(seed), 17)
    return {
        "stream_in": draw_stream_in(jax.random.fold_in(keys[16], 71), 0),
        "attention_gain": jnp.clip(1.0 + 0.1 * jax.random.normal(keys[1], (DEPTH_NUMBER, D), jnp.float32), 0.5, 1.5),
        "feedforward_gain": jnp.clip(1.0 + 0.1 * jax.random.normal(keys[2], (DEPTH_NUMBER, D), jnp.float32), 0.5, 1.5),
        "final_gain": jnp.clip(1.0 + 0.1 * jax.random.normal(keys[3], (D,), jnp.float32), 0.5, 1.5),
        "qkv_weight": normal_values(keys[4], (DEPTH_NUMBER, D, PORTION_FOCI * 3 * HEAD), D ** -0.5, 0.15625, ((1, 4), (2, 8))),
        "forget_weight": normal_values(keys[5], (DEPTH_NUMBER, D, PORTION_FOCI), D ** -0.5, 0.15625, ((1, 4), (2, 8))),
        "forget_bias": jnp.clip(-2.0 + 5.0 * jax.random.uniform(keys[6], (DEPTH_NUMBER, PORTION_FOCI), jnp.float32) ** block_scale(keys[6], (DEPTH_NUMBER, PORTION_FOCI), ((1, 8),), -0.2, 0.2), -2.0, 3.0),
        "out_weight": normal_values(keys[7], (DEPTH_NUMBER, PORTION_FOCI * HEAD, D), (PORTION_FOCI * HEAD) ** -0.5, 0.1875, ((1, 8), (2, 4))),
        "gate_weight": normal_values(keys[8], (DEPTH_NUMBER, D, FF), D ** -0.5, 0.15625, ((1, 4), (2, 8))),
        "up_weight": normal_values(keys[9], (DEPTH_NUMBER, D, FF), D ** -0.5, 0.15625, ((1, 4), (2, 8))),
        "down_weight": normal_values(keys[10], (DEPTH_NUMBER, FF, D), FF ** -0.5, 0.09375, ((1, 8), (2, 4))),
        "head_weight": normal_values(keys[11], (D, VOCAB), D ** -0.5, 0.15625, ((0, 4), (1, 8))),
        "kv_cache": draw_kv_cache(jax.random.fold_in(keys[16], 71), 0),
        "decay_cache": draw_decay_cache(jax.random.fold_in(keys[16], 71), 0),
        "lengths": draw_lengths(jax.random.fold_in(keys[16], 71), 0),
        "page_table": draw_page_table(jax.random.fold_in(keys[16], 71), 0),
    }


SCORE_SCALE = 0.125
NEGATIVE = -1e+30
EPSILON = 1e-06

def slot_layout(lengths, page_table, slot_count):
    request_count, page_count = page_table.shape
    request_ids = jnp.broadcast_to(jnp.arange(request_count, dtype=jnp.int32)[:, None], (request_count, page_count))
    page_ids = jnp.broadcast_to(jnp.arange(page_count, dtype=jnp.int32)[None, :], (request_count, page_count))
    targets = jnp.where(page_table >= 0, page_table, slot_count).reshape(-1)
    slot_owner = jnp.full((slot_count,), -1, jnp.int32).at[targets].set(request_ids.reshape(-1), mode='drop')
    page_index = jnp.zeros((slot_count,), jnp.int32).at[targets].set(page_ids.reshape(-1), mode='drop')
    safe_owner = jnp.maximum(slot_owner, 0)
    covered = lengths[safe_owner] - page_index * SHEET_ENTRIES
    offsets = jnp.arange(SHEET_ENTRIES, dtype=jnp.int32)
    live_slots = (slot_owner[:, None] >= 0) & (offsets[None, :] < covered[:, None])
    return (slot_owner, live_slots)

def normalize(stream, gain):
    mean_square = lax.optimization_barrier(jnp.mean(stream * stream, axis=1))
    rms_value = jnp.sqrt(mean_square + EPSILON)
    return ((stream / rms_value[:, None] * gain[None, :]).astype(jnp.bfloat16), rms_value)

def attend(queries, new_keys, new_values, forget_log, kv_layer, decay_layer, slot_owner, live_slots):
    request_count = queries.shape[0]
    safe_owner = jnp.maximum(slot_owner, 0)
    valid_page = slot_owner >= 0
    outputs = []
    for head_id in range(PORTION_FOCI):
        cache_keys = kv_layer[:, :, head_id, :HEAD].astype(jnp.float32)
        cache_values = kv_layer[:, :, head_id, HEAD:].astype(jnp.float32)
        query_rows = queries[:, head_id, :].astype(jnp.float32)
        scores = jnp.einsum('pd,ptd->pt', query_rows[safe_owner], cache_keys) * SCORE_SCALE
        scores = scores + decay_layer[:, head_id, :] + forget_log[safe_owner, head_id][:, None]
        scores = jnp.where(live_slots, scores, NEGATIVE)
        own_score = lax.optimization_barrier(jnp.sum(query_rows * new_keys[:, head_id, :].astype(jnp.float32), axis=1)) * SCORE_SCALE
        page_peak = jnp.where(valid_page, lax.optimization_barrier(jnp.max(scores, axis=1)), NEGATIVE)
        row_peak = jnp.full((request_count,), NEGATIVE, jnp.float32).at[safe_owner].max(page_peak)
        row_peak = jnp.maximum(row_peak, own_score)
        weights = jnp.where(live_slots, jnp.exp(scores - row_peak[safe_owner][:, None]), 0.0)
        rounded = lax.optimization_barrier(weights.astype(jnp.bfloat16)).astype(jnp.float32)
        page_sums = jnp.einsum('pt,ptd->pd', rounded, cache_values)
        numerator = jnp.zeros((request_count, HEAD), jnp.float32).at[safe_owner].add(page_sums)
        denominator = jnp.zeros((request_count,), jnp.float32).at[safe_owner].add(lax.optimization_barrier(jnp.sum(weights, axis=1)))
        own_weight = jnp.exp(own_score - row_peak)
        own_rounded = lax.optimization_barrier(own_weight.astype(jnp.bfloat16)).astype(jnp.float32)
        numerator = numerator + own_rounded[:, None] * new_values[:, head_id, :].astype(jnp.float32)
        denominator = denominator + own_weight
        outputs.append(numerator / denominator[:, None])
    return jnp.stack(outputs, axis=1).reshape(request_count, PORTION_FOCI * HEAD).astype(jnp.bfloat16)

def reference(stream_in, attention_gain, feedforward_gain, final_gain, qkv_weight, forget_weight, forget_bias, out_weight, gate_weight, up_weight, down_weight, head_weight, kv_cache, decay_cache, lengths, page_table):
    slot_owner, live_slots = slot_layout(lengths, page_table, SHEETS_OVERALL)
    request_count = stream_in.shape[0]
    stream = stream_in.astype(jnp.float32)
    for layer_id in range(DEPTH_NUMBER):
        normed, unused_rms = normalize(stream, attention_gain[layer_id])
        projected = jnp.dot(normed, qkv_weight[layer_id], preferred_element_type=jnp.float32)
        projected = projected.reshape(request_count, PORTION_FOCI, 3 * HEAD)
        queries = projected[:, :, :HEAD].astype(jnp.bfloat16)
        new_keys = projected[:, :, HEAD:2 * HEAD].astype(jnp.bfloat16)
        new_values = projected[:, :, 2 * HEAD:].astype(jnp.bfloat16)
        forget_logit = jnp.dot(normed, forget_weight[layer_id], preferred_element_type=jnp.float32)
        forget_log = jax.nn.log_sigmoid(forget_logit + forget_bias[layer_id][None, :])
        attended = attend(queries, new_keys, new_values, forget_log, kv_cache[layer_id], decay_cache[layer_id], slot_owner, live_slots)
        stream = stream + jnp.dot(attended, out_weight[layer_id], preferred_element_type=jnp.float32)
        normed, unused_rms = normalize(stream, feedforward_gain[layer_id])
        gate_part = jnp.dot(normed, gate_weight[layer_id], preferred_element_type=jnp.float32)
        up_part = jnp.dot(normed, up_weight[layer_id], preferred_element_type=jnp.float32)
        hidden = (jax.nn.silu(gate_part) * up_part).astype(jnp.bfloat16)
        stream = stream + jnp.dot(hidden, down_weight[layer_id], preferred_element_type=jnp.float32)
    final_hidden, row_norms = normalize(stream, final_gain)
    logits = jnp.dot(final_hidden, head_weight, preferred_element_type=jnp.float32)
    return (final_hidden, row_norms, lax.optimization_barrier(jnp.max(logits, axis=1)))
```

```python
import jax
import jax.numpy as jnp
from jax import lax
from jax.sharding import PartitionSpec as P

HEAD = 64
DEPTH_NUMBER = 2
SHEET_ENTRIES = 128

SCORE_SCALE = 0.125
NEGATIVE = -1e30
EPSILON = 1e-06
LOW_BLOCK = 16


def gather_sum(value, axis):
    return jnp.sum(lax.all_gather(value, axis), axis=0)


def local_slots(page_table, base, slot_count):
    request_count, page_count = page_table.shape
    flat = page_table.reshape(-1) - base
    valid = (flat >= 0) & (flat < slot_count)
    high = jnp.where(valid, flat // LOW_BLOCK, -1)
    low = flat % LOW_BLOCK
    entry = jnp.arange(request_count * page_count, dtype=jnp.int32)
    owner_code = (entry // page_count + 1).astype(jnp.float32)
    page_code = (entry % page_count).astype(jnp.float32)
    high_count = slot_count // LOW_BLOCK
    high_hot = (high[None, :] == jnp.arange(high_count, dtype=jnp.int32)[:, None]).astype(jnp.float32)
    low_hot = (low[None, :] == jnp.arange(LOW_BLOCK, dtype=jnp.int32)[:, None]).astype(jnp.bfloat16)
    coded = jnp.concatenate(
        [high_hot * owner_code[None, :], high_hot * page_code[None, :]], axis=0
    ).astype(jnp.bfloat16)
    table = lax.dot_general(
        coded, low_hot, (((1,), (1,)), ((), ())), preferred_element_type=jnp.float32
    )
    table = table.reshape(2, slot_count).astype(jnp.int32)
    owner = table[0] - 1
    page = table[1]
    return owner, page


def local_attention(queries, forget_log, kv_layer, decay_layer, owner, live, member):
    slots, tokens, heads, width = kv_layer.shape
    request_count = queries.shape[0]
    safe_owner = jnp.maximum(owner, 0)
    kv_flat = kv_layer.reshape(slots, tokens, heads * width)
    slot_queries = queries[safe_owner]
    padded = jnp.concatenate([slot_queries, jnp.zeros_like(slot_queries)], axis=2)
    diagonal = jnp.eye(heads, dtype=jnp.bfloat16)
    query_block = (diagonal[None, :, :, None] * padded[:, :, None, :]).reshape(
        slots, heads, heads * width
    )
    scores = jnp.einsum(
        "ptc,phc->pht", kv_flat, query_block, preferred_element_type=jnp.float32
    ) * SCORE_SCALE
    scores = scores + decay_layer + forget_log[safe_owner][:, :, None]
    scores = jnp.where(live[:, None, :], scores, NEGATIVE)
    page_peak = jnp.max(scores, axis=2)
    row_peak = jnp.max(jnp.where(member[:, :, None], page_peak[None], NEGATIVE), axis=1)
    slot_peak = row_peak[safe_owner]
    weights = jnp.where(live[:, None, :], jnp.exp(scores - slot_peak[:, :, None]), 0.0)
    page_sum = jnp.sum(weights, axis=2)
    mixed = jnp.einsum(
        "pht,ptc->phc", weights.astype(jnp.bfloat16), kv_flat, preferred_element_type=jnp.float32
    ).reshape(slots, heads, heads, width)
    page_out = jnp.stack([mixed[:, h, h, HEAD:] for h in range(heads)], axis=1)
    member_f = member.astype(jnp.float32)
    row_sum = jnp.einsum("rp,ph->rh", member_f, page_sum, precision=lax.Precision.HIGHEST)
    row_out = jnp.einsum("rp,phd->rhd", member_f, page_out, precision=lax.Precision.HIGHEST)
    return row_peak, row_sum, row_out


def merge_pages(row_peak, row_sum, row_out):
    packed = jnp.concatenate([row_peak[:, :, None], row_sum[:, :, None], row_out], axis=2)
    every = lax.all_gather(packed, "gx")
    peaks = every[:, :, :, 0]
    top = jnp.max(peaks, axis=0)
    scale = jnp.exp(peaks - top[None])
    total = jnp.sum(scale * every[:, :, :, 1], axis=0)
    out = jnp.sum(scale[..., None] * every[:, :, :, 2:], axis=0)
    return top, total, out


def local(
    stream_in,
    attention_gain,
    feedforward_gain,
    final_gain,
    qkv_weight,
    forget_weight,
    forget_bias,
    out_weight,
    gate_weight,
    up_weight,
    down_weight,
    head_weight,
    kv_cache,
    decay_cache,
    lengths,
    page_table,
):
    local_pages = kv_cache.shape[1]
    local_heads = kv_cache.shape[3]
    request_count = stream_in.shape[0]
    width = stream_in.shape[1] * lax.axis_size("gx")
    base = lax.axis_index("gx") * local_pages
    owner, page = local_slots(page_table, base, local_pages)
    member = owner[None, :] == jnp.arange(request_count, dtype=jnp.int32)[:, None]
    slot_length = jnp.sum(jnp.where(member, lengths[:, None], 0), axis=0)
    offsets = jnp.arange(SHEET_ENTRIES, dtype=jnp.int32)
    live = (owner[:, None] >= 0) & (
        page[:, None] * SHEET_ENTRIES + offsets[None, :] < slot_length[:, None]
    )
    stream = stream_in.astype(jnp.float32)
    qkv_cols = qkv_weight.shape[2]
    for layer_id in range(DEPTH_NUMBER):
        squares = jnp.sum(stream * stream, axis=1)
        scaled = (stream * attention_gain[layer_id][None, :]).astype(jnp.bfloat16)
        qkv_part = jnp.dot(scaled, qkv_weight[layer_id], preferred_element_type=jnp.float32)
        forget_part = jnp.dot(scaled, forget_weight[layer_id], preferred_element_type=jnp.float32)
        total = gather_sum(
            jnp.concatenate([qkv_part, forget_part, squares[:, None]], axis=1), "gx"
        )
        rms_value = jnp.sqrt(total[:, -1] / width + EPSILON)
        projected = (total[:, :qkv_cols] / rms_value[:, None]).reshape(
            request_count, local_heads, 3 * HEAD
        )
        forget_logit = total[:, qkv_cols : qkv_cols + local_heads] / rms_value[:, None]
        queries = projected[:, :, :HEAD].astype(jnp.bfloat16)
        new_keys = projected[:, :, HEAD : 2 * HEAD].astype(jnp.bfloat16)
        new_values = projected[:, :, 2 * HEAD :].astype(jnp.bfloat16)
        forget_log = jax.nn.log_sigmoid(forget_logit + forget_bias[layer_id][None, :])
        local_peak, local_sum, local_out = local_attention(
            queries, forget_log, kv_cache[layer_id], decay_cache[layer_id], owner, live, member
        )
        row_peak, row_sum, row_out = merge_pages(local_peak, local_sum, local_out)
        own_score = (
            jnp.sum(queries.astype(jnp.float32) * new_keys.astype(jnp.float32), axis=2)
            * SCORE_SCALE
        )
        full_peak = jnp.maximum(row_peak, own_score)
        cache_scale = jnp.exp(row_peak - full_peak)
        own_weight = jnp.exp(own_score - full_peak)
        own_rounded = lax.optimization_barrier(own_weight.astype(jnp.bfloat16)).astype(jnp.float32)
        numerator = cache_scale[:, :, None] * row_out + own_rounded[:, :, None] * new_values.astype(
            jnp.float32
        )
        denominator = cache_scale * row_sum + own_weight
        attended = (
            (numerator / denominator[:, :, None])
            .reshape(request_count, local_heads * HEAD)
            .astype(jnp.bfloat16)
        )
        stream = stream + gather_sum(
            jnp.dot(attended, out_weight[layer_id], preferred_element_type=jnp.float32), "gy"
        )
        squares = jnp.sum(stream * stream, axis=1)
        scaled = (stream * feedforward_gain[layer_id][None, :]).astype(jnp.bfloat16)
        gate_part = jnp.dot(scaled, gate_weight[layer_id], preferred_element_type=jnp.float32)
        up_part = jnp.dot(scaled, up_weight[layer_id], preferred_element_type=jnp.float32)
        hidden_cols = gate_part.shape[1]
        total = gather_sum(jnp.concatenate([gate_part, squares[:, None]], axis=1), "gx")
        up_total = gather_sum(up_part, "gx")
        rms_value = jnp.sqrt(total[:, -1] / width + EPSILON)
        gate_full = total[:, :hidden_cols] / rms_value[:, None]
        up_full = up_total / rms_value[:, None]
        hidden = (jax.nn.silu(gate_full) * up_full).astype(jnp.bfloat16)
        stream = stream + gather_sum(
            jnp.dot(hidden, down_weight[layer_id], preferred_element_type=jnp.float32), "gy"
        )
    squares = jnp.sum(stream * stream, axis=1)
    scaled = (stream * final_gain[None, :]).astype(jnp.bfloat16)
    logits = jnp.dot(scaled, head_weight, preferred_element_type=jnp.float32)
    parts = lax.axis_size("gx")
    chunk = logits.shape[1] // parts
    pieces = jnp.concatenate(
        [
            logits.reshape(request_count, parts, chunk),
            jnp.broadcast_to(squares[:, None, None], (request_count, parts, 1)),
        ],
        axis=2,
    )
    pieces = jnp.sum(lax.all_to_all(pieces, "gx", 1, 1, tiled=True), axis=1)
    rms_value = jnp.sqrt(pieces[:, chunk] / width + EPSILON)
    final_hidden = (stream / rms_value[:, None] * final_gain[None, :]).astype(jnp.bfloat16)
    local_top = jnp.max(pieces[:, :chunk], axis=1) / rms_value
    top_logits = lax.pmax(local_top, ("gx", "gy"))
    return (final_hidden, rms_value, top_logits)


def solution(mesh):
    placed = (
        P(None, "gx"),
        P(None, "gx"),
        P(None, "gx"),
        P("gx"),
        P(None, "gx", "gy"),
        P(None, "gx", "gy"),
        P(None, "gy"),
        P(None, "gy", "gx"),
        P(None, "gx", "gy"),
        P(None, "gx", "gy"),
        P(None, "gy", "gx"),
        P("gx", "gy"),
        P(None, "gx", None, "gy", None),
        P(None, "gx", "gy", None),
        P(),
        P(),
    )
    return jax.shard_map(
        local, mesh=mesh, in_specs=placed, out_specs=(P(None, "gx"), P(), P()), check_vma=False
    )
```

```python
import jax
import jax.numpy as jnp
from jax import lax
from jax.sharding import PartitionSpec as P

HEAD = 64
DEPTH_NUMBER = 2
SHEET_ENTRIES = 128

SCORE_SCALE = 0.125
NEGATIVE = -1e30
EPSILON = 1e-06
LOW_BLOCK = 16


def gather_sum(value, axis):
    return jnp.sum(lax.all_gather(value, axis), axis=0)


def local_slots(page_table, base, slot_count):
    request_count, page_count = page_table.shape
    flat = page_table.reshape(-1) - base
    valid = (flat >= 0) & (flat < slot_count)
    high = jnp.where(valid, flat // LOW_BLOCK, -1)
    low = flat % LOW_BLOCK
    entry = jnp.arange(request_count * page_count, dtype=jnp.int32)
    owner_code = (entry // page_count + 1).astype(jnp.float32)
    page_code = (entry % page_count).astype(jnp.float32)
    high_count = slot_count // LOW_BLOCK
    high_hot = (high[None, :] == jnp.arange(high_count, dtype=jnp.int32)[:, None]).astype(jnp.float32)
    low_hot = (low[None, :] == jnp.arange(LOW_BLOCK, dtype=jnp.int32)[:, None]).astype(jnp.bfloat16)
    coded = jnp.concatenate(
        [high_hot * owner_code[None, :], high_hot * page_code[None, :]], axis=0
    ).astype(jnp.bfloat16)
    table = lax.dot_general(
        coded, low_hot, (((1,), (1,)), ((), ())), preferred_element_type=jnp.float32
    )
    table = table.reshape(2, slot_count).astype(jnp.int32)
    owner = table[0] - 1
    page = table[1]
    return owner, page


def local_attention(queries, forget_log, kv_layer, decay_layer, owner, live, member):
    slots, tokens, heads, width = kv_layer.shape
    safe_owner = jnp.maximum(owner, 0)
    slot_queries = queries[safe_owner]
    padded = jnp.concatenate([slot_queries, jnp.zeros_like(slot_queries)], axis=2)
    diagonal = jnp.eye(heads, dtype=jnp.bfloat16)
    query_block = diagonal[None, :, :, None] * padded[:, :, None, :]
    scores = jnp.einsum(
        "pthc,pkhc->pkt", kv_layer, query_block, preferred_element_type=jnp.float32
    ) * SCORE_SCALE
    scores = scores + decay_layer + forget_log[safe_owner][:, :, None]
    scores = jnp.where(live[:, None, :], scores, NEGATIVE)
    page_peak = jnp.max(scores, axis=2)
    row_peak = jnp.max(jnp.where(member[:, :, None], page_peak[None], NEGATIVE), axis=1)
    slot_peak = row_peak[safe_owner]
    weights = jnp.where(live[:, None, :], jnp.exp(scores - slot_peak[:, :, None]), 0.0)
    page_sum = jnp.sum(weights, axis=2)
    mixed = jnp.einsum(
        "pkt,pthc->pkhc", weights.astype(jnp.bfloat16), kv_layer, preferred_element_type=jnp.float32
    )
    page_out = jnp.stack([mixed[:, h, h, HEAD:] for h in range(heads)], axis=1)
    member_f = member.astype(jnp.float32)
    row_sum = jnp.einsum("rp,ph->rh", member_f, page_sum, precision=lax.Precision.HIGHEST)
    row_out = jnp.einsum("rp,phd->rhd", member_f, page_out, precision=lax.Precision.HIGHEST)
    return row_peak, row_sum, row_out


def merge_pages(row_peak, row_sum, row_out):
    packed = jnp.concatenate([row_peak[:, :, None], row_sum[:, :, None], row_out], axis=2)
    every = lax.all_gather(packed, "gx")
    peaks = every[:, :, :, 0]
    top = jnp.max(peaks, axis=0)
    scale = jnp.exp(peaks - top[None])
    total = jnp.sum(scale * every[:, :, :, 1], axis=0)
    out = jnp.sum(scale[..., None] * every[:, :, :, 2:], axis=0)
    return top, total, out


def local(
    stream_in,
    attention_gain,
    feedforward_gain,
    final_gain,
    qkv_weight,
    forget_weight,
    forget_bias,
    out_weight,
    gate_weight,
    up_weight,
    down_weight,
    head_weight,
    kv_cache,
    decay_cache,
    lengths,
    page_table,
):
    local_pages = kv_cache.shape[1]
    local_heads = kv_cache.shape[3]
    request_count = stream_in.shape[0]
    width = stream_in.shape[1] * lax.axis_size("gx")
    base = lax.axis_index("gx") * local_pages
    owner, page = local_slots(page_table, base, local_pages)
    member = owner[None, :] == jnp.arange(request_count, dtype=jnp.int32)[:, None]
    slot_length = jnp.sum(jnp.where(member, lengths[:, None], 0), axis=0)
    offsets = jnp.arange(SHEET_ENTRIES, dtype=jnp.int32)
    live = (owner[:, None] >= 0) & (
        page[:, None] * SHEET_ENTRIES + offsets[None, :] < slot_length[:, None]
    )
    stream = stream_in.astype(jnp.float32)
    qkv_cols = qkv_weight.shape[2]
    for layer_id in range(DEPTH_NUMBER):
        squares = jnp.sum(stream * stream, axis=1)
        scaled = (stream * attention_gain[layer_id][None, :]).astype(jnp.bfloat16)
        qkv_part = jnp.dot(scaled, qkv_weight[layer_id], preferred_element_type=jnp.float32)
        forget_part = jnp.dot(scaled, forget_weight[layer_id], preferred_element_type=jnp.float32)
        total = gather_sum(
            jnp.concatenate([qkv_part, forget_part, squares[:, None]], axis=1), "gx"
        )
        rms_value = jnp.sqrt(total[:, -1] / width + EPSILON)
        projected = (total[:, :qkv_cols] / rms_value[:, None]).reshape(
            request_count, local_heads, 3 * HEAD
        )
        forget_logit = total[:, qkv_cols : qkv_cols + local_heads] / rms_value[:, None]
        queries = projected[:, :, :HEAD].astype(jnp.bfloat16)
        new_keys = projected[:, :, HEAD : 2 * HEAD].astype(jnp.bfloat16)
        new_values = projected[:, :, 2 * HEAD :].astype(jnp.bfloat16)
        forget_log = jax.nn.log_sigmoid(forget_logit + forget_bias[layer_id][None, :])
        local_peak, local_sum, local_out = local_attention(
            queries, forget_log, kv_cache[layer_id], decay_cache[layer_id], owner, live, member
        )
        row_peak, row_sum, row_out = merge_pages(local_peak, local_sum, local_out)
        own_score = (
            jnp.sum(queries.astype(jnp.float32) * new_keys.astype(jnp.float32), axis=2)
            * SCORE_SCALE
        )
        full_peak = jnp.maximum(row_peak, own_score)
        cache_scale = jnp.exp(row_peak - full_peak)
        own_weight = jnp.exp(own_score - full_peak)
        own_rounded = lax.optimization_barrier(own_weight.astype(jnp.bfloat16)).astype(jnp.float32)
        numerator = cache_scale[:, :, None] * row_out + own_rounded[:, :, None] * new_values.astype(
            jnp.float32
        )
        denominator = cache_scale * row_sum + own_weight
        attended = (
            (numerator / denominator[:, :, None])
            .reshape(request_count, local_heads * HEAD)
            .astype(jnp.bfloat16)
        )
        stream = stream + gather_sum(
            jnp.dot(attended, out_weight[layer_id], preferred_element_type=jnp.float32), "gy"
        )
        squares = jnp.sum(stream * stream, axis=1)
        scaled = (stream * feedforward_gain[layer_id][None, :]).astype(jnp.bfloat16)
        gate_part = jnp.dot(scaled, gate_weight[layer_id], preferred_element_type=jnp.float32)
        up_part = jnp.dot(scaled, up_weight[layer_id], preferred_element_type=jnp.float32)
        hidden_cols = gate_part.shape[1]
        total = gather_sum(jnp.concatenate([gate_part, squares[:, None]], axis=1), "gx")
        up_total = gather_sum(up_part, "gx")
        rms_value = jnp.sqrt(total[:, -1] / width + EPSILON)
        gate_full = total[:, :hidden_cols] / rms_value[:, None]
        up_full = up_total / rms_value[:, None]
        hidden = (jax.nn.silu(gate_full) * up_full).astype(jnp.bfloat16)
        stream = stream + gather_sum(
            jnp.dot(hidden, down_weight[layer_id], preferred_element_type=jnp.float32), "gy"
        )
    squares = jnp.sum(stream * stream, axis=1)
    scaled = (stream * final_gain[None, :]).astype(jnp.bfloat16)
    logits = jnp.dot(scaled, head_weight, preferred_element_type=jnp.float32)
    parts = lax.axis_size("gx")
    chunk = logits.shape[1] // parts
    pieces = jnp.concatenate(
        [
            logits.reshape(request_count, parts, chunk),
            jnp.broadcast_to(squares[:, None, None], (request_count, parts, 1)),
        ],
        axis=2,
    )
    pieces = jnp.sum(lax.all_to_all(pieces, "gx", 1, 1, tiled=True), axis=1)
    rms_value = jnp.sqrt(pieces[:, chunk] / width + EPSILON)
    final_hidden = (stream / rms_value[:, None] * final_gain[None, :]).astype(jnp.bfloat16)
    local_top = jnp.max(pieces[:, :chunk], axis=1) / rms_value
    top_logits = lax.pmax(lax.pmax(local_top, "gx"), "gy")
    return (final_hidden, rms_value, top_logits)


def solution(mesh):
    placed = (
        P(None, "gx"),
        P(None, "gx"),
        P(None, "gx"),
        P("gx"),
        P(None, "gx", "gy"),
        P(None, "gx", "gy"),
        P(None, "gy"),
        P(None, "gy", "gx"),
        P(None, "gx", "gy"),
        P(None, "gx", "gy"),
        P(None, "gy", "gx"),
        P("gx", "gy"),
        P(None, "gx", None, "gy", None),
        P(None, "gx", "gy", None),
        P(),
        P(),
    )
    return jax.shard_map(
        local, mesh=mesh, in_specs=placed, out_specs=(P(None, "gx"), P(), P()), check_vma=False
    )
```

```python
import jax
import jax.numpy as jnp
from jax import lax
from jax.sharding import PartitionSpec as P

HEAD = 64
DEPTH_NUMBER = 2
SHEET_ENTRIES = 128

SCORE_SCALE = 0.125
NEGATIVE = -1e30
EPSILON = 1e-06
LOW_BLOCK = 16


def gather_sum(value, axis):
    return jnp.sum(lax.all_gather(value, axis), axis=0)


def xor_sum(value, axis):
    count = lax.axis_size(axis)
    parts = [value] + [
        lax.ppermute(value, axis, [(i, i ^ k) for i in range(count)]) for k in range(1, count)
    ]
    while len(parts) > 1:
        parts = [parts[i] + parts[i + 1] for i in range(0, len(parts), 2)]
    return parts[0]


def local_slots(page_table, base, slot_count):
    request_count, page_count = page_table.shape
    flat = page_table.reshape(-1) - base
    valid = (flat >= 0) & (flat < slot_count)
    high = jnp.where(valid, flat // LOW_BLOCK, -1)
    low = flat % LOW_BLOCK
    entry = jnp.arange(request_count * page_count, dtype=jnp.int32)
    owner_code = (entry // page_count + 1).astype(jnp.float32)
    page_code = (entry % page_count).astype(jnp.float32)
    high_count = slot_count // LOW_BLOCK
    high_hot = (high[None, :] == jnp.arange(high_count, dtype=jnp.int32)[:, None]).astype(jnp.float32)
    low_hot = (low[None, :] == jnp.arange(LOW_BLOCK, dtype=jnp.int32)[:, None]).astype(jnp.bfloat16)
    coded = jnp.concatenate(
        [high_hot * owner_code[None, :], high_hot * page_code[None, :]], axis=0
    ).astype(jnp.bfloat16)
    table = lax.dot_general(
        coded, low_hot, (((1,), (1,)), ((), ())), preferred_element_type=jnp.float32
    )
    table = table.reshape(2, slot_count).astype(jnp.int32)
    owner = table[0] - 1
    page = table[1]
    return owner, page


def local_attention(queries, forget_log, kv_layer, decay_layer, owner, live, member):
    slots, tokens, heads, width = kv_layer.shape
    safe_owner = jnp.maximum(owner, 0)
    slot_queries = queries[safe_owner]
    padded = jnp.concatenate([slot_queries, jnp.zeros_like(slot_queries)], axis=2)
    diagonal = jnp.eye(heads, dtype=jnp.bfloat16)
    query_block = diagonal[None, :, :, None] * padded[:, :, None, :]
    scores = jnp.einsum(
        "pthc,pkhc->pkt", kv_layer, query_block, preferred_element_type=jnp.float32
    ) * SCORE_SCALE
    scores = scores + decay_layer + forget_log[safe_owner][:, :, None]
    scores = jnp.where(live[:, None, :], scores, NEGATIVE)
    page_peak = jnp.max(scores, axis=2)
    row_peak = jnp.max(jnp.where(member[:, :, None], page_peak[None], NEGATIVE), axis=1)
    slot_peak = row_peak[safe_owner]
    weights = jnp.where(live[:, None, :], jnp.exp(scores - slot_peak[:, :, None]), 0.0)
    page_sum = jnp.sum(weights, axis=2)
    mixed = jnp.einsum(
        "pkt,pthc->pkhc", weights.astype(jnp.bfloat16), kv_layer, preferred_element_type=jnp.float32
    )
    page_out = jnp.stack([mixed[:, h, h, HEAD:] for h in range(heads)], axis=1)
    member_f = member.astype(jnp.float32)
    row_sum = jnp.einsum("rp,ph->rh", member_f, page_sum, precision=lax.Precision.HIGHEST)
    row_out = jnp.einsum("rp,phd->rhd", member_f, page_out, precision=lax.Precision.HIGHEST)
    return row_peak, row_sum, row_out


def merge_pages(row_peak, row_sum, row_out):
    packed = jnp.concatenate([row_peak[:, :, None], row_sum[:, :, None], row_out], axis=2)
    every = lax.all_gather(packed, "gx")
    peaks = every[:, :, :, 0]
    top = jnp.max(peaks, axis=0)
    scale = jnp.exp(peaks - top[None])
    total = jnp.sum(scale * every[:, :, :, 1], axis=0)
    out = jnp.sum(scale[..., None] * every[:, :, :, 2:], axis=0)
    return top, total, out


def local(
    stream_in,
    attention_gain,
    feedforward_gain,
    final_gain,
    qkv_weight,
    forget_weight,
    forget_bias,
    out_weight,
    gate_weight,
    up_weight,
    down_weight,
    head_weight,
    kv_cache,
    decay_cache,
    lengths,
    page_table,
):
    local_pages = kv_cache.shape[1]
    local_heads = kv_cache.shape[3]
    request_count = stream_in.shape[0]
    width = stream_in.shape[1] * lax.axis_size("gx")
    base = lax.axis_index("gx") * local_pages
    owner, page = local_slots(page_table, base, local_pages)
    member = owner[None, :] == jnp.arange(request_count, dtype=jnp.int32)[:, None]
    slot_length = jnp.sum(jnp.where(member, lengths[:, None], 0), axis=0)
    offsets = jnp.arange(SHEET_ENTRIES, dtype=jnp.int32)
    live = (owner[:, None] >= 0) & (
        page[:, None] * SHEET_ENTRIES + offsets[None, :] < slot_length[:, None]
    )
    stream = stream_in.astype(jnp.float32)
    qkv_cols = qkv_weight.shape[2]
    for layer_id in range(DEPTH_NUMBER):
        squares = jnp.sum(stream * stream, axis=1)
        scaled = (stream * attention_gain[layer_id][None, :]).astype(jnp.bfloat16)
        qkv_part = jnp.dot(scaled, qkv_weight[layer_id], preferred_element_type=jnp.float32)
        forget_part = jnp.dot(scaled, forget_weight[layer_id], preferred_element_type=jnp.float32)
        total = xor_sum(
            jnp.concatenate([qkv_part, forget_part, squares[:, None]], axis=1), "gx"
        )
        rms_value = jnp.sqrt(total[:, -1] / width + EPSILON)
        projected = (total[:, :qkv_cols] / rms_value[:, None]).reshape(
            request_count, local_heads, 3 * HEAD
        )
        forget_logit = total[:, qkv_cols : qkv_cols + local_heads] / rms_value[:, None]
        queries = projected[:, :, :HEAD].astype(jnp.bfloat16)
        new_keys = projected[:, :, HEAD : 2 * HEAD].astype(jnp.bfloat16)
        new_values = projected[:, :, 2 * HEAD :].astype(jnp.bfloat16)
        forget_log = jax.nn.log_sigmoid(forget_logit + forget_bias[layer_id][None, :])
        local_peak, local_sum, local_out = local_attention(
            queries, forget_log, kv_cache[layer_id], decay_cache[layer_id], owner, live, member
        )
        row_peak, row_sum, row_out = merge_pages(local_peak, local_sum, local_out)
        own_score = (
            jnp.sum(queries.astype(jnp.float32) * new_keys.astype(jnp.float32), axis=2)
            * SCORE_SCALE
        )
        full_peak = jnp.maximum(row_peak, own_score)
        cache_scale = jnp.exp(row_peak - full_peak)
        own_weight = jnp.exp(own_score - full_peak)
        own_rounded = lax.optimization_barrier(own_weight.astype(jnp.bfloat16)).astype(jnp.float32)
        numerator = cache_scale[:, :, None] * row_out + own_rounded[:, :, None] * new_values.astype(
            jnp.float32
        )
        denominator = cache_scale * row_sum + own_weight
        attended = (
            (numerator / denominator[:, :, None])
            .reshape(request_count, local_heads * HEAD)
            .astype(jnp.bfloat16)
        )
        stream = stream + gather_sum(
            jnp.dot(attended, out_weight[layer_id], preferred_element_type=jnp.float32), "gy"
        )
        squares = jnp.sum(stream * stream, axis=1)
        scaled = (stream * feedforward_gain[layer_id][None, :]).astype(jnp.bfloat16)
        gate_part = jnp.dot(scaled, gate_weight[layer_id], preferred_element_type=jnp.float32)
        up_part = jnp.dot(scaled, up_weight[layer_id], preferred_element_type=jnp.float32)
        hidden_cols = gate_part.shape[1]
        total = xor_sum(jnp.concatenate([gate_part, up_part, squares[:, None]], axis=1), "gx")
        rms_value = jnp.sqrt(total[:, -1] / width + EPSILON)
        gate_full = total[:, :hidden_cols] / rms_value[:, None]
        up_full = total[:, hidden_cols : 2 * hidden_cols] / rms_value[:, None]
        hidden = (jax.nn.silu(gate_full) * up_full).astype(jnp.bfloat16)
        stream = stream + gather_sum(
            jnp.dot(hidden, down_weight[layer_id], preferred_element_type=jnp.float32), "gy"
        )
    squares = jnp.sum(stream * stream, axis=1)
    scaled = (stream * final_gain[None, :]).astype(jnp.bfloat16)
    logits = jnp.dot(scaled, head_weight, preferred_element_type=jnp.float32)
    parts = lax.axis_size("gx")
    chunk = logits.shape[1] // parts
    squares_high = squares.astype(jnp.bfloat16)
    squares_low = (squares - squares_high.astype(jnp.float32)).astype(jnp.bfloat16)
    squares_pair = jnp.stack([squares_high, squares_low], axis=1)
    pieces = jnp.concatenate(
        [
            logits.astype(jnp.bfloat16).reshape(request_count, parts, chunk),
            jnp.broadcast_to(squares_pair[:, None, :], (request_count, parts, 2)),
        ],
        axis=2,
    )
    pieces = lax.all_to_all(pieces, "gx", 1, 1, tiled=True).astype(jnp.float32)
    top_part = jnp.sum(pieces[:, :, :chunk], axis=1)
    total_squares = jnp.sum(pieces[:, :, chunk] + pieces[:, :, chunk + 1], axis=1)
    rms_value = jnp.sqrt(total_squares / width + EPSILON)
    final_hidden = (stream / rms_value[:, None] * final_gain[None, :]).astype(jnp.bfloat16)
    local_top = jnp.max(top_part, axis=1) / rms_value
    top_logits = lax.pmax(lax.pmax(local_top, "gx"), "gy")
    return (final_hidden, rms_value, top_logits)


def solution(mesh):
    placed = (
        P(None, "gx"),
        P(None, "gx"),
        P(None, "gx"),
        P("gx"),
        P(None, "gx", "gy"),
        P(None, "gx", "gy"),
        P(None, "gy"),
        P(None, "gy", "gx"),
        P(None, "gx", "gy"),
        P(None, "gx", "gy"),
        P(None, "gy", "gx"),
        P("gx", "gy"),
        P(None, "gx", None, "gy", None),
        P(None, "gx", "gy", None),
        P(),
        P(),
    )
    return jax.shard_map(
        local, mesh=mesh, in_specs=placed, out_specs=(P(None, "gx"), P(), P()), check_vma=False
    )
```

```python
import jax
import jax.numpy as jnp
from jax import lax
from jax.sharding import PartitionSpec as P

HEAD = 64
DEPTH_NUMBER = 2
SHEET_ENTRIES = 128

SCORE_SCALE = 0.125
NEGATIVE = -1e30
EPSILON = 1e-06
LOW_BLOCK = 16


def gather_sum(value, axis):
    return jnp.sum(lax.all_gather(value, axis), axis=0)


def xor_sum(value, axis, kind=None):
    count = lax.axis_size(axis)
    parts = [value] + [
        lax.ppermute(value, axis, [(i, i ^ k) for i in range(count)]) for k in range(1, count)
    ]
    if kind is not None:
        parts = [part.astype(kind) for part in parts]
    while len(parts) > 1:
        parts = [parts[i] + parts[i + 1] for i in range(0, len(parts), 2)]
    return parts[0]


def split_pair(value):
    high = value.astype(jnp.bfloat16)
    low = (value - high.astype(jnp.float32)).astype(jnp.bfloat16)
    return jnp.stack([high, low], axis=1)


def xor_max(value, axis):
    count = lax.axis_size(axis)
    parts = [value] + [
        lax.ppermute(value, axis, [(i, i ^ k) for i in range(count)]) for k in range(1, count)
    ]
    while len(parts) > 1:
        parts = [jnp.maximum(parts[i], parts[i + 1]) for i in range(0, len(parts), 2)]
    return parts[0]


def local_slots(page_table, base, slot_count):
    request_count, page_count = page_table.shape
    flat = page_table.reshape(-1) - base
    valid = (flat >= 0) & (flat < slot_count)
    high = jnp.where(valid, flat // LOW_BLOCK, -1)
    low = flat % LOW_BLOCK
    entry = jnp.arange(request_count * page_count, dtype=jnp.int32)
    owner_code = (entry // page_count + 1).astype(jnp.float32)
    page_code = (entry % page_count).astype(jnp.float32)
    high_count = slot_count // LOW_BLOCK
    high_hot = (high[None, :] == jnp.arange(high_count, dtype=jnp.int32)[:, None]).astype(jnp.float32)
    low_hot = (low[None, :] == jnp.arange(LOW_BLOCK, dtype=jnp.int32)[:, None]).astype(jnp.bfloat16)
    coded = jnp.concatenate(
        [high_hot * owner_code[None, :], high_hot * page_code[None, :]], axis=0
    ).astype(jnp.bfloat16)
    table = lax.dot_general(
        coded, low_hot, (((1,), (1,)), ((), ())), preferred_element_type=jnp.float32
    )
    table = table.reshape(2, slot_count).astype(jnp.int32)
    owner = table[0] - 1
    page = table[1]
    return owner, page


def local_attention(queries, forget_log, kv_layer, decay_layer, owner, live, member):
    slots, tokens, heads, width = kv_layer.shape
    safe_owner = jnp.maximum(owner, 0)
    slot_queries = queries[safe_owner]
    padded = jnp.concatenate([slot_queries, jnp.zeros_like(slot_queries)], axis=2)
    diagonal = jnp.eye(heads, dtype=jnp.bfloat16)
    query_block = diagonal[None, :, :, None] * padded[:, :, None, :]
    scores = jnp.einsum(
        "pthc,pkhc->pkt", kv_layer, query_block, preferred_element_type=jnp.float32
    ) * SCORE_SCALE
    scores = scores + decay_layer + forget_log[safe_owner][:, :, None]
    scores = jnp.where(live[:, None, :], scores, NEGATIVE)
    page_peak = jnp.max(scores, axis=2)
    row_peak = jnp.max(jnp.where(member[:, :, None], page_peak[None], NEGATIVE), axis=1)
    slot_peak = row_peak[safe_owner]
    weights = jnp.where(live[:, None, :], jnp.exp(scores - slot_peak[:, :, None]), 0.0)
    page_sum = jnp.sum(weights, axis=2)
    mixed = jnp.einsum(
        "pkt,pthc->pkhc", weights.astype(jnp.bfloat16), kv_layer, preferred_element_type=jnp.float32
    )
    page_out = jnp.stack([mixed[:, h, h, HEAD:] for h in range(heads)], axis=1)
    member_f = member.astype(jnp.float32)
    row_sum = jnp.einsum("rp,ph->rh", member_f, page_sum, precision=lax.Precision.HIGHEST)
    row_out = jnp.einsum("rp,phd->rhd", member_f, page_out, precision=lax.Precision.HIGHEST)
    return row_peak, row_sum, row_out


def merge_pages(row_peak, row_sum, row_out):
    packed = jnp.concatenate([row_peak[:, :, None], row_sum[:, :, None], row_out], axis=2)
    every = lax.all_gather(packed, "gx")
    peaks = every[:, :, :, 0]
    top = jnp.max(peaks, axis=0)
    scale = jnp.exp(peaks - top[None])
    total = jnp.sum(scale * every[:, :, :, 1], axis=0)
    out = jnp.sum(scale[..., None] * every[:, :, :, 2:], axis=0)
    return top, total, out


def local(
    stream_in,
    attention_gain,
    feedforward_gain,
    final_gain,
    qkv_weight,
    forget_weight,
    forget_bias,
    out_weight,
    gate_weight,
    up_weight,
    down_weight,
    head_weight,
    kv_cache,
    decay_cache,
    lengths,
    page_table,
):
    local_pages = kv_cache.shape[1]
    local_heads = kv_cache.shape[3]
    request_count = stream_in.shape[0]
    width = stream_in.shape[1] * lax.axis_size("gx")
    base = lax.axis_index("gx") * local_pages
    owner, page = local_slots(page_table, base, local_pages)
    member = owner[None, :] == jnp.arange(request_count, dtype=jnp.int32)[:, None]
    slot_length = jnp.sum(jnp.where(member, lengths[:, None], 0), axis=0)
    offsets = jnp.arange(SHEET_ENTRIES, dtype=jnp.int32)
    live = (owner[:, None] >= 0) & (
        page[:, None] * SHEET_ENTRIES + offsets[None, :] < slot_length[:, None]
    )
    stream = stream_in.astype(jnp.float32)
    qkv_cols = qkv_weight.shape[2]
    for layer_id in range(DEPTH_NUMBER):
        squares = jnp.sum(stream * stream, axis=1)
        scaled = (stream * attention_gain[layer_id][None, :]).astype(jnp.bfloat16)
        qkv_part = jnp.dot(scaled, qkv_weight[layer_id], preferred_element_type=jnp.float32)
        forget_part = jnp.dot(scaled, forget_weight[layer_id], preferred_element_type=jnp.float32)
        total = xor_sum(
            jnp.concatenate(
                [qkv_part.astype(jnp.bfloat16), forget_part.astype(jnp.bfloat16), split_pair(squares)],
                axis=1,
            ),
            "gx",
            jnp.float32,
        )
        rms_value = jnp.sqrt((total[:, -2] + total[:, -1]) / width + EPSILON)
        projected = (total[:, :qkv_cols] / rms_value[:, None]).reshape(
            request_count, local_heads, 3 * HEAD
        )
        forget_logit = total[:, qkv_cols : qkv_cols + local_heads] / rms_value[:, None]
        queries = projected[:, :, :HEAD].astype(jnp.bfloat16)
        new_keys = projected[:, :, HEAD : 2 * HEAD].astype(jnp.bfloat16)
        new_values = projected[:, :, 2 * HEAD :].astype(jnp.bfloat16)
        forget_log = jax.nn.log_sigmoid(forget_logit + forget_bias[layer_id][None, :])
        local_peak, local_sum, local_out = local_attention(
            queries, forget_log, kv_cache[layer_id], decay_cache[layer_id], owner, live, member
        )
        row_peak, row_sum, row_out = merge_pages(local_peak, local_sum, local_out)
        own_score = (
            jnp.sum(queries.astype(jnp.float32) * new_keys.astype(jnp.float32), axis=2)
            * SCORE_SCALE
        )
        full_peak = jnp.maximum(row_peak, own_score)
        cache_scale = jnp.exp(row_peak - full_peak)
        own_weight = jnp.exp(own_score - full_peak)
        own_rounded = lax.optimization_barrier(own_weight.astype(jnp.bfloat16)).astype(jnp.float32)
        numerator = cache_scale[:, :, None] * row_out + own_rounded[:, :, None] * new_values.astype(
            jnp.float32
        )
        denominator = cache_scale * row_sum + own_weight
        attended = (
            (numerator / denominator[:, :, None])
            .reshape(request_count, local_heads * HEAD)
            .astype(jnp.bfloat16)
        )
        stream = stream + gather_sum(
            jnp.dot(attended, out_weight[layer_id], preferred_element_type=jnp.float32), "gy"
        )
        squares = jnp.sum(stream * stream, axis=1)
        scaled = (stream * feedforward_gain[layer_id][None, :]).astype(jnp.bfloat16)
        gate_part = jnp.dot(scaled, gate_weight[layer_id], preferred_element_type=jnp.float32)
        up_part = jnp.dot(scaled, up_weight[layer_id], preferred_element_type=jnp.float32)
        hidden_cols = gate_part.shape[1]
        total = xor_sum(
            jnp.concatenate(
                [gate_part.astype(jnp.bfloat16), up_part.astype(jnp.bfloat16), split_pair(squares)],
                axis=1,
            ),
            "gx",
            jnp.float32,
        )
        rms_value = jnp.sqrt((total[:, -2] + total[:, -1]) / width + EPSILON)
        gate_full = total[:, :hidden_cols] / rms_value[:, None]
        up_full = total[:, hidden_cols : 2 * hidden_cols] / rms_value[:, None]
        hidden = (jax.nn.silu(gate_full) * up_full).astype(jnp.bfloat16)
        stream = stream + gather_sum(
            jnp.dot(hidden, down_weight[layer_id], preferred_element_type=jnp.float32), "gy"
        )
    squares = jnp.sum(stream * stream, axis=1)
    scaled = (stream * final_gain[None, :]).astype(jnp.bfloat16)
    logits = jnp.dot(scaled, head_weight, preferred_element_type=jnp.float32)
    parts = lax.axis_size("gx")
    chunk = logits.shape[1] // parts
    squares_pair = split_pair(squares)
    pieces = jnp.concatenate(
        [
            logits.astype(jnp.bfloat16).reshape(request_count, parts, chunk),
            jnp.broadcast_to(squares_pair[:, None, :], (request_count, parts, 2)),
        ],
        axis=2,
    )
    pieces = lax.all_to_all(pieces, "gx", 1, 1, tiled=True).astype(jnp.float32)
    top_part = jnp.sum(pieces[:, :, :chunk], axis=1)
    total_squares = jnp.sum(pieces[:, :, chunk] + pieces[:, :, chunk + 1], axis=1)
    rms_value = jnp.sqrt(total_squares / width + EPSILON)
    final_hidden = (stream / rms_value[:, None] * final_gain[None, :]).astype(jnp.bfloat16)
    local_top = jnp.max(top_part, axis=1) / rms_value
    top_logits = xor_max(lax.pmax(local_top, "gx"), "gy")
    return (final_hidden, rms_value, top_logits)


def solution(mesh):
    placed = (
        P(None, "gx"),
        P(None, "gx"),
        P(None, "gx"),
        P("gx"),
        P(None, "gx", "gy"),
        P(None, "gx", "gy"),
        P(None, "gy"),
        P(None, "gy", "gx"),
        P(None, "gx", "gy"),
        P(None, "gx", "gy"),
        P(None, "gy", "gx"),
        P("gx", "gy"),
        P(None, "gx", None, "gy", None),
        P(None, "gx", "gy", None),
        P(),
        P(),
    )
    return jax.shard_map(
        local, mesh=mesh, in_specs=placed, out_specs=(P(None, "gx"), P(), P()), check_vma=False
    )
```

```python
import jax
import jax.numpy as jnp
from jax import lax
from jax.sharding import PartitionSpec as P

HEAD = 64
DEPTH_NUMBER = 2
SHEET_ENTRIES = 128

SCORE_SCALE = 0.125
NEGATIVE = -1e30
EPSILON = 1e-06
LOW_BLOCK = 16


def gather_sum(value, axis):
    return jnp.sum(lax.all_gather(value, axis).astype(jnp.float32), axis=0)


def xor_sum(value, axis, kind=None):
    count = lax.axis_size(axis)
    parts = [value] + [
        lax.ppermute(value, axis, [(i, i ^ k) for i in range(count)]) for k in range(1, count)
    ]
    if kind is not None:
        parts = [part.astype(kind) for part in parts]
    while len(parts) > 1:
        parts = [parts[i] + parts[i + 1] for i in range(0, len(parts), 2)]
    return parts[0]


def butterfly(parts, join):
    while len(parts) > 1:
        parts = [join(parts[i], parts[i + 1]) for i in range(0, len(parts), 2)]
    return parts[0]


def exchange(value, axis, partner):
    count = lax.axis_size(axis)
    return lax.ppermute(value, axis, [(i, i ^ partner) for i in range(count)])


def core_first_sum(value, axis):
    carried = value.astype(jnp.bfloat16)
    pair = carried.astype(jnp.float32) + exchange(carried, axis, 1).astype(jnp.float32)
    pair = pair.astype(jnp.bfloat16)
    count = lax.axis_size(axis)
    parts = [pair] + [exchange(pair, axis, k) for k in range(2, count, 2)]
    return butterfly([part.astype(jnp.float32) for part in parts], jnp.add)


def split_pair(value):
    high = value.astype(jnp.bfloat16)
    low = (value - high.astype(jnp.float32)).astype(jnp.bfloat16)
    return jnp.stack([high, low], axis=1)


def xor_max(value, axis):
    count = lax.axis_size(axis)
    parts = [value] + [
        lax.ppermute(value, axis, [(i, i ^ k) for i in range(count)]) for k in range(1, count)
    ]
    while len(parts) > 1:
        parts = [jnp.maximum(parts[i], parts[i + 1]) for i in range(0, len(parts), 2)]
    return parts[0]


def local_slots(page_table, base, slot_count):
    request_count, page_count = page_table.shape
    flat = page_table.reshape(-1) - base
    valid = (flat >= 0) & (flat < slot_count)
    high = jnp.where(valid, flat // LOW_BLOCK, -1)
    low = flat % LOW_BLOCK
    entry = jnp.arange(request_count * page_count, dtype=jnp.int32)
    owner_code = (entry // page_count + 1).astype(jnp.float32)
    page_code = (entry % page_count).astype(jnp.float32)
    high_count = slot_count // LOW_BLOCK
    high_hot = (high[None, :] == jnp.arange(high_count, dtype=jnp.int32)[:, None]).astype(jnp.float32)
    low_hot = (low[None, :] == jnp.arange(LOW_BLOCK, dtype=jnp.int32)[:, None]).astype(jnp.bfloat16)
    coded = jnp.concatenate(
        [high_hot * owner_code[None, :], high_hot * page_code[None, :]], axis=0
    ).astype(jnp.bfloat16)
    table = lax.dot_general(
        coded, low_hot, (((1,), (1,)), ((), ())), preferred_element_type=jnp.float32
    )
    table = table.reshape(2, slot_count).astype(jnp.int32)
    owner = table[0] - 1
    page = table[1]
    return owner, page


def local_attention(queries, forget_log, kv_layer, decay_layer, owner, live, member):
    slots, tokens, heads, width = kv_layer.shape
    safe_owner = jnp.maximum(owner, 0)
    slot_queries = queries[safe_owner]
    padded = jnp.concatenate([slot_queries, jnp.zeros_like(slot_queries)], axis=2)
    diagonal = jnp.eye(heads, dtype=jnp.bfloat16)
    query_block = diagonal[None, :, :, None] * padded[:, :, None, :]
    scores = jnp.einsum(
        "pthc,pkhc->pkt", kv_layer, query_block, preferred_element_type=jnp.float32
    ) * SCORE_SCALE
    scores = scores + decay_layer + forget_log[safe_owner][:, :, None]
    scores = jnp.where(live[:, None, :], scores, NEGATIVE)
    page_peak = jnp.max(scores, axis=2)
    row_peak = jnp.max(jnp.where(member[:, :, None], page_peak[None], NEGATIVE), axis=1)
    slot_peak = row_peak[safe_owner]
    weights = jnp.where(live[:, None, :], jnp.exp(scores - slot_peak[:, :, None]), 0.0)
    page_sum = jnp.sum(weights, axis=2)
    mixed = jnp.einsum(
        "pkt,pthc->pkhc", weights.astype(jnp.bfloat16), kv_layer, preferred_element_type=jnp.float32
    )
    page_out = jnp.stack([mixed[:, h, h, HEAD:] for h in range(heads)], axis=1)
    member_f = member.astype(jnp.float32)
    row_sum = jnp.einsum("rp,ph->rh", member_f, page_sum, precision=lax.Precision.HIGHEST)
    row_out = jnp.einsum("rp,phd->rhd", member_f, page_out, precision=lax.Precision.HIGHEST)
    return row_peak, row_sum, row_out


def merge_pages(row_peak, row_sum, row_out):
    packed = jnp.concatenate([row_peak[:, :, None], row_sum[:, :, None], row_out], axis=2)
    count = lax.axis_size("gx")
    every = [packed] + [exchange(packed, "gx", k) for k in range(1, count)]
    top = butterfly([part[:, :, 0] for part in every], jnp.maximum)
    scales = [jnp.exp(part[:, :, 0] - top) for part in every]
    total = butterfly([scale * part[:, :, 1] for scale, part in zip(scales, every)], jnp.add)
    out = butterfly(
        [scale[..., None] * part[:, :, 2:] for scale, part in zip(scales, every)], jnp.add
    )
    return top, total, out


def local(
    stream_in,
    attention_gain,
    feedforward_gain,
    final_gain,
    qkv_weight,
    forget_weight,
    forget_bias,
    out_weight,
    gate_weight,
    up_weight,
    down_weight,
    head_weight,
    kv_cache,
    decay_cache,
    lengths,
    page_table,
):
    local_pages = kv_cache.shape[1]
    local_heads = kv_cache.shape[3]
    request_count = stream_in.shape[0]
    width = stream_in.shape[1] * lax.axis_size("gx")
    base = lax.axis_index("gx") * local_pages
    owner, page = local_slots(page_table, base, local_pages)
    member = owner[None, :] == jnp.arange(request_count, dtype=jnp.int32)[:, None]
    slot_length = jnp.sum(jnp.where(member, lengths[:, None], 0), axis=0)
    offsets = jnp.arange(SHEET_ENTRIES, dtype=jnp.int32)
    live = (owner[:, None] >= 0) & (
        page[:, None] * SHEET_ENTRIES + offsets[None, :] < slot_length[:, None]
    )
    stream = stream_in.astype(jnp.float32)
    qkv_cols = qkv_weight.shape[2]
    for layer_id in range(DEPTH_NUMBER):
        squares = jnp.sum(stream * stream, axis=1)
        scaled = (stream * attention_gain[layer_id][None, :]).astype(jnp.bfloat16)
        qkv_part = jnp.dot(scaled, qkv_weight[layer_id], preferred_element_type=jnp.float32)
        forget_part = jnp.dot(scaled, forget_weight[layer_id], preferred_element_type=jnp.float32)
        total = xor_sum(
            jnp.concatenate(
                [qkv_part.astype(jnp.bfloat16), forget_part.astype(jnp.bfloat16), split_pair(squares)],
                axis=1,
            ),
            "gx",
            jnp.float32,
        )
        rms_value = jnp.sqrt((total[:, -2] + total[:, -1]) / width + EPSILON)
        projected = (total[:, :qkv_cols] / rms_value[:, None]).reshape(
            request_count, local_heads, 3 * HEAD
        )
        forget_logit = total[:, qkv_cols : qkv_cols + local_heads] / rms_value[:, None]
        queries = projected[:, :, :HEAD].astype(jnp.bfloat16)
        new_keys = projected[:, :, HEAD : 2 * HEAD].astype(jnp.bfloat16)
        new_values = projected[:, :, 2 * HEAD :].astype(jnp.bfloat16)
        forget_log = jax.nn.log_sigmoid(forget_logit + forget_bias[layer_id][None, :])
        local_peak, local_sum, local_out = local_attention(
            queries, forget_log, kv_cache[layer_id], decay_cache[layer_id], owner, live, member
        )
        row_peak, row_sum, row_out = merge_pages(local_peak, local_sum, local_out)
        own_score = (
            jnp.sum(queries.astype(jnp.float32) * new_keys.astype(jnp.float32), axis=2)
            * SCORE_SCALE
        )
        full_peak = jnp.maximum(row_peak, own_score)
        cache_scale = jnp.exp(row_peak - full_peak)
        own_weight = jnp.exp(own_score - full_peak)
        own_rounded = lax.optimization_barrier(own_weight.astype(jnp.bfloat16)).astype(jnp.float32)
        numerator = cache_scale[:, :, None] * row_out + own_rounded[:, :, None] * new_values.astype(
            jnp.float32
        )
        denominator = cache_scale * row_sum + own_weight
        attended = (
            (numerator / denominator[:, :, None])
            .reshape(request_count, local_heads * HEAD)
            .astype(jnp.bfloat16)
        )
        stream = stream + core_first_sum(
            jnp.dot(attended, out_weight[layer_id], preferred_element_type=jnp.float32), "gy"
        )
        squares = jnp.sum(stream * stream, axis=1)
        scaled = (stream * feedforward_gain[layer_id][None, :]).astype(jnp.bfloat16)
        gate_part = jnp.dot(scaled, gate_weight[layer_id], preferred_element_type=jnp.float32)
        up_part = jnp.dot(scaled, up_weight[layer_id], preferred_element_type=jnp.float32)
        hidden_cols = gate_part.shape[1]
        total = gather_sum(
            jnp.concatenate(
                [gate_part.astype(jnp.bfloat16), up_part.astype(jnp.bfloat16), split_pair(squares)],
                axis=1,
            ),
            "gx",
        )
        rms_value = jnp.sqrt((total[:, -2] + total[:, -1]) / width + EPSILON)
        gate_full = total[:, :hidden_cols] / rms_value[:, None]
        up_full = total[:, hidden_cols : 2 * hidden_cols] / rms_value[:, None]
        hidden = (jax.nn.silu(gate_full) * up_full).astype(jnp.bfloat16)
        stream = stream + core_first_sum(
            jnp.dot(hidden, down_weight[layer_id], preferred_element_type=jnp.float32), "gy"
        )
    squares = jnp.sum(stream * stream, axis=1)
    scaled = (stream * final_gain[None, :]).astype(jnp.bfloat16)
    logits = jnp.dot(scaled, head_weight, preferred_element_type=jnp.float32)
    parts = lax.axis_size("gx")
    chunk = logits.shape[1] // parts
    squares_pair = split_pair(squares)
    pieces = jnp.concatenate(
        [
            logits.astype(jnp.bfloat16).reshape(request_count, parts, chunk),
            jnp.broadcast_to(squares_pair[:, None, :], (request_count, parts, 2)),
        ],
        axis=2,
    )
    pieces = lax.all_to_all(pieces, "gx", 1, 1, tiled=True).astype(jnp.float32)
    top_part = jnp.sum(pieces[:, :, :chunk], axis=1)
    total_squares = jnp.sum(pieces[:, :, chunk] + pieces[:, :, chunk + 1], axis=1)
    rms_value = jnp.sqrt(total_squares / width + EPSILON)
    final_hidden = (stream / rms_value[:, None] * final_gain[None, :]).astype(jnp.bfloat16)
    local_top = jnp.max(top_part, axis=1) / rms_value
    top_logits = xor_max(lax.pmax(local_top, "gx"), "gy")
    return (final_hidden, rms_value, top_logits)


def solution(mesh):
    placed = (
        P(None, "gx"),
        P(None, "gx"),
        P(None, "gx"),
        P("gx"),
        P(None, "gx", "gy"),
        P(None, "gx", "gy"),
        P(None, "gy"),
        P(None, "gy", "gx"),
        P(None, "gx", "gy"),
        P(None, "gx", "gy"),
        P(None, "gy", "gx"),
        P("gx", "gy"),
        P(None, "gx", None, "gy", None),
        P(None, "gx", "gy", None),
        P(),
        P(),
    )
    return jax.shard_map(
        local, mesh=mesh, in_specs=placed, out_specs=(P(None, "gx"), P(), P()), check_vma=False
    )
```

```python
import jax
import jax.numpy as jnp
from jax import lax
from jax.sharding import PartitionSpec as P

HEAD = 64
DEPTH_NUMBER = 2
SHEET_ENTRIES = 128

SCORE_SCALE = 0.125
NEGATIVE = -1e30
EPSILON = 1e-06
LOW_BLOCK = 16


def gather_sum(value, axis):
    return jnp.sum(lax.all_gather(value, axis).astype(jnp.float32), axis=0)


def xor_sum(value, axis, kind=None):
    count = lax.axis_size(axis)
    parts = [value] + [
        lax.ppermute(value, axis, [(i, i ^ k) for i in range(count)]) for k in range(1, count)
    ]
    if kind is not None:
        parts = [part.astype(kind) for part in parts]
    while len(parts) > 1:
        parts = [parts[i] + parts[i + 1] for i in range(0, len(parts), 2)]
    return parts[0]


def butterfly(parts, join):
    while len(parts) > 1:
        parts = [join(parts[i], parts[i + 1]) for i in range(0, len(parts), 2)]
    return parts[0]


def exchange(value, axis, partner):
    count = lax.axis_size(axis)
    return lax.ppermute(value, axis, [(i, i ^ partner) for i in range(count)])


def core_first_sum(value, axis):
    carried = value.astype(jnp.bfloat16)
    pair = carried.astype(jnp.float32) + exchange(carried, axis, 1).astype(jnp.float32)
    pair = pair.astype(jnp.bfloat16)
    count = lax.axis_size(axis)
    parts = [pair] + [exchange(pair, axis, k) for k in range(2, count, 2)]
    return butterfly([part.astype(jnp.float32) for part in parts], jnp.add)


def core_first_max(value, axis):
    pair = jnp.maximum(value, exchange(value, axis, 1))
    count = lax.axis_size(axis)
    parts = [pair] + [exchange(pair, axis, k) for k in range(2, count, 2)]
    return butterfly(parts, jnp.maximum)


def split_pair(value):
    high = value.astype(jnp.bfloat16)
    low = (value - high.astype(jnp.float32)).astype(jnp.bfloat16)
    return jnp.stack([high, low], axis=1)


def xor_max(value, axis):
    count = lax.axis_size(axis)
    parts = [value] + [
        lax.ppermute(value, axis, [(i, i ^ k) for i in range(count)]) for k in range(1, count)
    ]
    while len(parts) > 1:
        parts = [jnp.maximum(parts[i], parts[i + 1]) for i in range(0, len(parts), 2)]
    return parts[0]


def local_slots(page_table, base, slot_count):
    request_count, page_count = page_table.shape
    flat = page_table.reshape(-1) - base
    valid = (flat >= 0) & (flat < slot_count)
    high = jnp.where(valid, flat // LOW_BLOCK, -1)
    low = flat % LOW_BLOCK
    entry = jnp.arange(request_count * page_count, dtype=jnp.int32)
    owner_code = (entry // page_count + 1).astype(jnp.float32)
    page_code = (entry % page_count).astype(jnp.float32)
    high_count = slot_count // LOW_BLOCK
    high_hot = (high[None, :] == jnp.arange(high_count, dtype=jnp.int32)[:, None]).astype(jnp.float32)
    low_hot = (low[None, :] == jnp.arange(LOW_BLOCK, dtype=jnp.int32)[:, None]).astype(jnp.bfloat16)
    coded = jnp.concatenate(
        [high_hot * owner_code[None, :], high_hot * page_code[None, :]], axis=0
    ).astype(jnp.bfloat16)
    table = lax.dot_general(
        coded, low_hot, (((1,), (1,)), ((), ())), preferred_element_type=jnp.float32
    )
    table = table.reshape(2, slot_count).astype(jnp.int32)
    owner = table[0] - 1
    page = table[1]
    return owner, page


def local_attention(queries, forget_log, kv_layer, decay_layer, owner, live, member):
    slots, tokens, heads, width = kv_layer.shape
    safe_owner = jnp.maximum(owner, 0)
    slot_queries = queries[safe_owner]
    padded = jnp.concatenate([slot_queries, jnp.zeros_like(slot_queries)], axis=2)
    diagonal = jnp.eye(heads, dtype=jnp.bfloat16)
    query_block = diagonal[None, :, :, None] * padded[:, :, None, :]
    scores = jnp.einsum(
        "pthc,pkhc->pkt", kv_layer, query_block, preferred_element_type=jnp.float32
    ) * SCORE_SCALE
    scores = scores + decay_layer + forget_log[safe_owner][:, :, None]
    scores = jnp.where(live[:, None, :], scores, NEGATIVE)
    page_peak = jnp.max(scores, axis=2)
    row_peak = jnp.max(jnp.where(member[:, :, None], page_peak[None], NEGATIVE), axis=1)
    slot_peak = row_peak[safe_owner]
    weights = jnp.where(live[:, None, :], jnp.exp(scores - slot_peak[:, :, None]), 0.0)
    page_sum = jnp.sum(weights, axis=2)
    mixed = jnp.einsum(
        "pkt,pthc->pkhc", weights.astype(jnp.bfloat16), kv_layer, preferred_element_type=jnp.float32
    )
    page_out = jnp.stack([mixed[:, h, h, HEAD:] for h in range(heads)], axis=1)
    member_f = member.astype(jnp.float32)
    row_sum = jnp.einsum("rp,ph->rh", member_f, page_sum, precision=lax.Precision.HIGHEST)
    row_out = jnp.einsum("rp,phd->rhd", member_f, page_out, precision=lax.Precision.HIGHEST)
    return row_peak, row_sum, row_out


def merge_pages(row_peak, row_sum, row_out):
    packed = jnp.concatenate([row_peak[:, :, None], row_sum[:, :, None], row_out], axis=2)
    count = lax.axis_size("gx")
    every = [packed] + [exchange(packed, "gx", k) for k in range(1, count)]
    top = butterfly([part[:, :, 0] for part in every], jnp.maximum)
    scales = [jnp.exp(part[:, :, 0] - top) for part in every]
    total = butterfly([scale * part[:, :, 1] for scale, part in zip(scales, every)], jnp.add)
    out = butterfly(
        [scale[..., None] * part[:, :, 2:] for scale, part in zip(scales, every)], jnp.add
    )
    return top, total, out


def local(
    stream_in,
    attention_gain,
    feedforward_gain,
    final_gain,
    qkv_weight,
    forget_weight,
    forget_bias,
    out_weight,
    gate_weight,
    up_weight,
    down_weight,
    head_weight,
    kv_cache,
    decay_cache,
    lengths,
    page_table,
):
    local_pages = kv_cache.shape[1]
    local_heads = kv_cache.shape[3]
    request_count = stream_in.shape[0]
    width = stream_in.shape[1] * lax.axis_size("gx")
    base = lax.axis_index("gx") * local_pages
    owner, page = local_slots(page_table, base, local_pages)
    member = owner[None, :] == jnp.arange(request_count, dtype=jnp.int32)[:, None]
    slot_length = jnp.sum(jnp.where(member, lengths[:, None], 0), axis=0)
    offsets = jnp.arange(SHEET_ENTRIES, dtype=jnp.int32)
    live = (owner[:, None] >= 0) & (
        page[:, None] * SHEET_ENTRIES + offsets[None, :] < slot_length[:, None]
    )
    stream = stream_in.astype(jnp.float32)
    qkv_cols = qkv_weight.shape[2]
    for layer_id in range(DEPTH_NUMBER):
        squares = jnp.sum(stream * stream, axis=1)
        scaled = (stream * attention_gain[layer_id][None, :]).astype(jnp.bfloat16)
        qkv_part = jnp.dot(scaled, qkv_weight[layer_id], preferred_element_type=jnp.float32)
        forget_part = jnp.dot(scaled, forget_weight[layer_id], preferred_element_type=jnp.float32)
        total = xor_sum(
            jnp.concatenate(
                [qkv_part.astype(jnp.bfloat16), forget_part.astype(jnp.bfloat16), split_pair(squares)],
                axis=1,
            ),
            "gx",
            jnp.float32,
        )
        rms_value = jnp.sqrt((total[:, -2] + total[:, -1]) / width + EPSILON)
        projected = (total[:, :qkv_cols] / rms_value[:, None]).reshape(
            request_count, local_heads, 3 * HEAD
        )
        forget_logit = total[:, qkv_cols : qkv_cols + local_heads] / rms_value[:, None]
        queries = projected[:, :, :HEAD].astype(jnp.bfloat16)
        new_keys = projected[:, :, HEAD : 2 * HEAD].astype(jnp.bfloat16)
        new_values = projected[:, :, 2 * HEAD :].astype(jnp.bfloat16)
        forget_log = jax.nn.log_sigmoid(forget_logit + forget_bias[layer_id][None, :])
        local_peak, local_sum, local_out = local_attention(
            queries, forget_log, kv_cache[layer_id], decay_cache[layer_id], owner, live, member
        )
        row_peak, row_sum, row_out = merge_pages(local_peak, local_sum, local_out)
        own_score = (
            jnp.sum(queries.astype(jnp.float32) * new_keys.astype(jnp.float32), axis=2)
            * SCORE_SCALE
        )
        full_peak = jnp.maximum(row_peak, own_score)
        cache_scale = jnp.exp(row_peak - full_peak)
        own_weight = jnp.exp(own_score - full_peak)
        own_rounded = lax.optimization_barrier(own_weight.astype(jnp.bfloat16)).astype(jnp.float32)
        numerator = cache_scale[:, :, None] * row_out + own_rounded[:, :, None] * new_values.astype(
            jnp.float32
        )
        denominator = cache_scale * row_sum + own_weight
        attended = (
            (numerator / denominator[:, :, None])
            .reshape(request_count, local_heads * HEAD)
            .astype(jnp.bfloat16)
        )
        stream = stream + core_first_sum(
            jnp.dot(attended, out_weight[layer_id], preferred_element_type=jnp.float32), "gy"
        )
        squares = jnp.sum(stream * stream, axis=1)
        scaled = (stream * feedforward_gain[layer_id][None, :]).astype(jnp.bfloat16)
        gate_part = jnp.dot(scaled, gate_weight[layer_id], preferred_element_type=jnp.float32)
        up_part = jnp.dot(scaled, up_weight[layer_id], preferred_element_type=jnp.float32)
        hidden_cols = gate_part.shape[1]
        total = gather_sum(
            jnp.concatenate(
                [gate_part.astype(jnp.bfloat16), up_part.astype(jnp.bfloat16), split_pair(squares)],
                axis=1,
            ),
            "gx",
        )
        rms_value = jnp.sqrt((total[:, -2] + total[:, -1]) / width + EPSILON)
        gate_full = total[:, :hidden_cols] / rms_value[:, None]
        up_full = total[:, hidden_cols : 2 * hidden_cols] / rms_value[:, None]
        hidden = (jax.nn.silu(gate_full) * up_full).astype(jnp.bfloat16)
        stream = stream + core_first_sum(
            jnp.dot(hidden, down_weight[layer_id], preferred_element_type=jnp.float32), "gy"
        )
    squares = jnp.sum(stream * stream, axis=1)
    scaled = (stream * final_gain[None, :]).astype(jnp.bfloat16)
    logits = jnp.dot(scaled, head_weight, preferred_element_type=jnp.float32)
    parts = lax.axis_size("gx")
    chunk = logits.shape[1] // parts
    squares_pair = split_pair(squares)
    pieces = jnp.concatenate(
        [
            logits.astype(jnp.bfloat16).reshape(request_count, parts, chunk),
            jnp.broadcast_to(squares_pair[:, None, :], (request_count, parts, 2)),
        ],
        axis=2,
    )
    pieces = lax.all_to_all(pieces, "gx", 1, 1, tiled=True).astype(jnp.float32)
    top_part = jnp.sum(pieces[:, :, :chunk], axis=1)
    total_squares = jnp.sum(pieces[:, :, chunk] + pieces[:, :, chunk + 1], axis=1)
    rms_value = jnp.sqrt(total_squares / width + EPSILON)
    final_hidden = (stream / rms_value[:, None] * final_gain[None, :]).astype(jnp.bfloat16)
    local_top = jnp.max(top_part, axis=1) / rms_value
    top_logits = core_first_max(xor_max(local_top, "gx"), "gy")
    return (final_hidden, rms_value, top_logits)


def solution(mesh):
    placed = (
        P(None, "gx"),
        P(None, "gx"),
        P(None, "gx"),
        P("gx"),
        P(None, "gx", "gy"),
        P(None, "gx", "gy"),
        P(None, "gy"),
        P(None, "gy", "gx"),
        P(None, "gx", "gy"),
        P(None, "gx", "gy"),
        P(None, "gy", "gx"),
        P("gx", "gy"),
        P(None, "gx", None, "gy", None),
        P(None, "gx", "gy", None),
        P(),
        P(),
    )
    return jax.shard_map(
        local, mesh=mesh, in_specs=placed, out_specs=(P(None, "gx"), P(), P()), check_vma=False
    )
```

```python
import jax
import jax.numpy as jnp
from jax import lax
from jax.sharding import PartitionSpec as P

HEAD = 64
DEPTH_NUMBER = 2
SHEET_ENTRIES = 128

SCORE_SCALE = 0.125
NEGATIVE = -1e30
EPSILON = 1e-06
LOW_BLOCK = 16


def gather_sum(value, axis):
    return jnp.sum(lax.all_gather(value, axis).astype(jnp.float32), axis=0)


def xor_sum(value, axis, kind=None):
    count = lax.axis_size(axis)
    parts = [value] + [
        lax.ppermute(value, axis, [(i, i ^ k) for i in range(count)]) for k in range(1, count)
    ]
    if kind is not None:
        parts = [part.astype(kind) for part in parts]
    while len(parts) > 1:
        parts = [parts[i] + parts[i + 1] for i in range(0, len(parts), 2)]
    return parts[0]


def butterfly(parts, join):
    while len(parts) > 1:
        parts = [join(parts[i], parts[i + 1]) for i in range(0, len(parts), 2)]
    return parts[0]


def exchange(value, axis, partner):
    count = lax.axis_size(axis)
    return lax.ppermute(value, axis, [(i, i ^ partner) for i in range(count)])


def core_first_sum(value, axis):
    carried = value.astype(jnp.bfloat16)
    pair = carried.astype(jnp.float32) + exchange(carried, axis, 1).astype(jnp.float32)
    pair = pair.astype(jnp.bfloat16)
    count = lax.axis_size(axis)
    parts = [pair] + [exchange(pair, axis, k) for k in range(2, count, 2)]
    return butterfly([part.astype(jnp.float32) for part in parts], jnp.add)


def core_first_max(value, axis):
    pair = jnp.maximum(value, exchange(value, axis, 1))
    count = lax.axis_size(axis)
    parts = [pair] + [exchange(pair, axis, k) for k in range(2, count, 2)]
    return butterfly(parts, jnp.maximum)


def split_pair(value):
    high = value.astype(jnp.bfloat16)
    low = (value - high.astype(jnp.float32)).astype(jnp.bfloat16)
    return jnp.stack([high, low], axis=1)


def xor_max(value, axis):
    count = lax.axis_size(axis)
    parts = [value] + [
        lax.ppermute(value, axis, [(i, i ^ k) for i in range(count)]) for k in range(1, count)
    ]
    while len(parts) > 1:
        parts = [jnp.maximum(parts[i], parts[i + 1]) for i in range(0, len(parts), 2)]
    return parts[0]


def local_slots(page_table, base, slot_count):
    request_count, page_count = page_table.shape
    flat = page_table.reshape(-1) - base
    valid = (flat >= 0) & (flat < slot_count)
    high = jnp.where(valid, flat // LOW_BLOCK, -1)
    low = flat % LOW_BLOCK
    entry = jnp.arange(request_count * page_count, dtype=jnp.int32)
    owner_code = (entry // page_count + 1).astype(jnp.float32)
    page_code = (entry % page_count).astype(jnp.float32)
    high_count = slot_count // LOW_BLOCK
    high_hot = (high[None, :] == jnp.arange(high_count, dtype=jnp.int32)[:, None]).astype(jnp.float32)
    low_hot = (low[None, :] == jnp.arange(LOW_BLOCK, dtype=jnp.int32)[:, None]).astype(jnp.bfloat16)
    coded = jnp.concatenate(
        [high_hot * owner_code[None, :], high_hot * page_code[None, :]], axis=0
    ).astype(jnp.bfloat16)
    table = lax.dot_general(
        coded, low_hot, (((1,), (1,)), ((), ())), preferred_element_type=jnp.float32
    )
    table = table.reshape(2, slot_count).astype(jnp.int32)
    owner = table[0] - 1
    page = table[1]
    return owner, page


def local_attention(queries, forget_log, kv_layer, decay_layer, owner, live, member):
    slots, tokens, heads, width = kv_layer.shape
    safe_owner = jnp.maximum(owner, 0)
    slot_queries = queries[safe_owner]
    padded = jnp.concatenate([slot_queries, jnp.zeros_like(slot_queries)], axis=2)
    diagonal = jnp.eye(heads, dtype=jnp.bfloat16)
    query_block = diagonal[None, :, :, None] * padded[:, :, None, :]
    scores = jnp.einsum(
        "pthc,pkhc->pkt", kv_layer, query_block, preferred_element_type=jnp.float32
    ) * SCORE_SCALE
    scores = scores + decay_layer + forget_log[safe_owner][:, :, None]
    scores = jnp.where(live[:, None, :], scores, NEGATIVE)
    page_peak = jnp.max(scores, axis=2)
    row_peak = jnp.max(jnp.where(member[:, :, None], page_peak[None], NEGATIVE), axis=1)
    slot_peak = row_peak[safe_owner]
    weights = jnp.where(live[:, None, :], jnp.exp(scores - slot_peak[:, :, None]), 0.0)
    page_sum = jnp.sum(weights, axis=2)
    mixed = jnp.einsum(
        "pkt,pthc->pkhc", weights.astype(jnp.bfloat16), kv_layer, preferred_element_type=jnp.float32
    )
    page_out = jnp.stack([mixed[:, h, h, HEAD:] for h in range(heads)], axis=1)
    member_f = member.astype(jnp.float32)
    row_sum = jnp.einsum("rp,ph->rh", member_f, page_sum, precision=lax.Precision.HIGHEST)
    row_out = jnp.einsum("rp,phd->rhd", member_f, page_out, precision=lax.Precision.HIGHEST)
    return row_peak, row_sum, row_out


def merge_pages(row_peak, row_sum, row_out):
    packed = jnp.concatenate([row_peak[:, :, None], row_sum[:, :, None], row_out], axis=2)
    count = lax.axis_size("gx")
    every = [packed] + [exchange(packed, "gx", k) for k in range(1, count)]
    top = butterfly([part[:, :, 0] for part in every], jnp.maximum)
    scales = [jnp.exp(part[:, :, 0] - top) for part in every]
    total = butterfly([scale * part[:, :, 1] for scale, part in zip(scales, every)], jnp.add)
    out = butterfly(
        [scale[..., None] * part[:, :, 2:] for scale, part in zip(scales, every)], jnp.add
    )
    return top, total, out


def local(
    stream_in,
    attention_gain,
    feedforward_gain,
    final_gain,
    qkv_weight,
    forget_weight,
    forget_bias,
    out_weight,
    gate_weight,
    up_weight,
    down_weight,
    head_weight,
    kv_cache,
    decay_cache,
    lengths,
    page_table,
):
    local_pages = kv_cache.shape[1]
    local_heads = kv_cache.shape[3]
    request_count = stream_in.shape[0]
    width = stream_in.shape[1] * lax.axis_size("gx")
    base = lax.axis_index("gx") * local_pages
    owner, page = local_slots(page_table, base, local_pages)
    member = owner[None, :] == jnp.arange(request_count, dtype=jnp.int32)[:, None]
    slot_length = jnp.sum(jnp.where(member, lengths[:, None], 0), axis=0)
    offsets = jnp.arange(SHEET_ENTRIES, dtype=jnp.int32)
    live = (owner[:, None] >= 0) & (
        page[:, None] * SHEET_ENTRIES + offsets[None, :] < slot_length[:, None]
    )
    stream = stream_in.astype(jnp.float32)
    qkv_cols = qkv_weight.shape[2]
    for layer_id in range(DEPTH_NUMBER):
        squares = jnp.sum(stream * stream, axis=1)
        scaled = (stream * attention_gain[layer_id][None, :]).astype(jnp.bfloat16)
        qkv_part = jnp.dot(scaled, qkv_weight[layer_id], preferred_element_type=jnp.float32)
        forget_part = jnp.dot(scaled, forget_weight[layer_id], preferred_element_type=jnp.float32)
        total = xor_sum(
            jnp.concatenate(
                [qkv_part.astype(jnp.bfloat16), forget_part.astype(jnp.bfloat16), split_pair(squares)],
                axis=1,
            ),
            "gx",
            jnp.float32,
        )
        rms_value = jnp.sqrt((total[:, -2] + total[:, -1]) / width + EPSILON)
        projected = (total[:, :qkv_cols] / rms_value[:, None]).reshape(
            request_count, local_heads, 3 * HEAD
        )
        forget_logit = total[:, qkv_cols : qkv_cols + local_heads] / rms_value[:, None]
        queries = projected[:, :, :HEAD].astype(jnp.bfloat16)
        new_keys = projected[:, :, HEAD : 2 * HEAD].astype(jnp.bfloat16)
        new_values = projected[:, :, 2 * HEAD :].astype(jnp.bfloat16)
        forget_log = jax.nn.log_sigmoid(forget_logit + forget_bias[layer_id][None, :])
        local_peak, local_sum, local_out = local_attention(
            queries, forget_log, kv_cache[layer_id], decay_cache[layer_id], owner, live, member
        )
        row_peak, row_sum, row_out = merge_pages(local_peak, local_sum, local_out)
        own_score = (
            jnp.sum(queries.astype(jnp.float32) * new_keys.astype(jnp.float32), axis=2)
            * SCORE_SCALE
        )
        full_peak = jnp.maximum(row_peak, own_score)
        cache_scale = jnp.exp(row_peak - full_peak)
        own_weight = jnp.exp(own_score - full_peak)
        own_rounded = lax.optimization_barrier(own_weight.astype(jnp.bfloat16)).astype(jnp.float32)
        numerator = cache_scale[:, :, None] * row_out + own_rounded[:, :, None] * new_values.astype(
            jnp.float32
        )
        denominator = cache_scale * row_sum + own_weight
        attended = (
            (numerator / denominator[:, :, None])
            .reshape(request_count, local_heads * HEAD)
            .astype(jnp.bfloat16)
        )
        stream = stream + core_first_sum(
            jnp.dot(attended, out_weight[layer_id], preferred_element_type=jnp.float32), "gy"
        )
        squares = jnp.sum(stream * stream, axis=1)
        scaled = (stream * feedforward_gain[layer_id][None, :]).astype(jnp.bfloat16)
        gate_part = jnp.dot(scaled, gate_weight[layer_id], preferred_element_type=jnp.float32)
        up_part = jnp.dot(scaled, up_weight[layer_id], preferred_element_type=jnp.float32)
        hidden_cols = gate_part.shape[1]
        total = gather_sum(
            jnp.concatenate(
                [gate_part.astype(jnp.bfloat16), up_part.astype(jnp.bfloat16), split_pair(squares)],
                axis=1,
            ),
            "gx",
        )
        rms_value = jnp.sqrt((total[:, -2] + total[:, -1]) / width + EPSILON)
        gate_full = total[:, :hidden_cols] / rms_value[:, None]
        up_full = total[:, hidden_cols : 2 * hidden_cols] / rms_value[:, None]
        hidden = (jax.nn.silu(gate_full) * up_full).astype(jnp.bfloat16)
        stream = stream + core_first_sum(
            jnp.dot(hidden, down_weight[layer_id], preferred_element_type=jnp.float32), "gy"
        )
    squares = jnp.sum(stream * stream, axis=1)
    scaled = (stream * final_gain[None, :]).astype(jnp.bfloat16)
    logits = jnp.dot(scaled, head_weight, preferred_element_type=jnp.float32)
    current = logits
    current_squares = squares
    position = lax.axis_index("gx")
    step = 1
    while step < lax.axis_size("gx"):
        half = current.shape[1] // 2
        side = (position // step) % 2
        keep = lax.dynamic_slice_in_dim(current, side * half, half, axis=1)
        send = lax.dynamic_slice_in_dim(current, (1 - side) * half, half, axis=1)
        pair = split_pair(current_squares)
        payload = jnp.concatenate([send.astype(jnp.bfloat16), pair], axis=1)
        got = exchange(payload, "gx", step).astype(jnp.float32)
        own_squares = pair[:, 0].astype(jnp.float32) + pair[:, 1].astype(jnp.float32)
        current_squares = own_squares + (got[:, half] + got[:, half + 1])
        current = keep + got[:, :half]
        step *= 2
    rms_value = jnp.sqrt(current_squares / width + EPSILON)
    final_hidden = (stream / rms_value[:, None] * final_gain[None, :]).astype(jnp.bfloat16)
    local_top = jnp.max(current, axis=1) / rms_value
    top_logits = core_first_max(xor_max(local_top, "gx"), "gy")
    return (final_hidden, rms_value, top_logits)


def solution(mesh):
    placed = (
        P(None, "gx"),
        P(None, "gx"),
        P(None, "gx"),
        P("gx"),
        P(None, "gx", "gy"),
        P(None, "gx", "gy"),
        P(None, "gy"),
        P(None, "gy", "gx"),
        P(None, "gx", "gy"),
        P(None, "gx", "gy"),
        P(None, "gy", "gx"),
        P("gx", "gy"),
        P(None, "gx", None, "gy", None),
        P(None, "gx", "gy", None),
        P(),
        P(),
    )
    return jax.shard_map(
        local, mesh=mesh, in_specs=placed, out_specs=(P(None, "gx"), P(), P()), check_vma=False
    )
```

```python
import jax
import jax.numpy as jnp
from jax import lax
from jax.sharding import PartitionSpec as P

HEAD = 64
DEPTH_NUMBER = 2
SHEET_ENTRIES = 128

SCORE_SCALE = 0.125
NEGATIVE = -1e30
EPSILON = 1e-06
LOW_BLOCK = 16


def gather_sum(value, axis):
    return jnp.sum(lax.all_gather(value, axis).astype(jnp.float32), axis=0)


def xor_sum(value, axis, kind=None):
    count = lax.axis_size(axis)
    parts = [value] + [
        lax.ppermute(value, axis, [(i, i ^ k) for i in range(count)]) for k in range(1, count)
    ]
    if kind is not None:
        parts = [part.astype(kind) for part in parts]
    while len(parts) > 1:
        parts = [parts[i] + parts[i + 1] for i in range(0, len(parts), 2)]
    return parts[0]


def gather_all(value, axis):
    count = lax.axis_size(axis)
    copies = jnp.broadcast_to(value[None], (count,) + value.shape)
    received = lax.all_to_all(copies, axis, 0, 0, tiled=True)
    return [received[k] for k in range(count)]


def butterfly(parts, join):
    while len(parts) > 1:
        parts = [join(parts[i], parts[i + 1]) for i in range(0, len(parts), 2)]
    return parts[0]


def exchange(value, axis, partner):
    count = lax.axis_size(axis)
    return lax.ppermute(value, axis, [(i, i ^ partner) for i in range(count)])


def core_first_sum(value, axis):
    carried = value.astype(jnp.bfloat16)
    pair = carried.astype(jnp.float32) + exchange(carried, axis, 1).astype(jnp.float32)
    pair = pair.astype(jnp.bfloat16)
    count = lax.axis_size(axis)
    parts = [pair] + [exchange(pair, axis, k) for k in range(2, count, 2)]
    return butterfly([part.astype(jnp.float32) for part in parts], jnp.add)


def core_first_max(value, axis):
    pair = jnp.maximum(value, exchange(value, axis, 1))
    count = lax.axis_size(axis)
    parts = [pair] + [exchange(pair, axis, k) for k in range(2, count, 2)]
    return butterfly(parts, jnp.maximum)


def split_pair(value):
    high = value.astype(jnp.bfloat16)
    low = (value - high.astype(jnp.float32)).astype(jnp.bfloat16)
    return jnp.stack([high, low], axis=1)


def xor_max(value, axis):
    count = lax.axis_size(axis)
    parts = [value] + [
        lax.ppermute(value, axis, [(i, i ^ k) for i in range(count)]) for k in range(1, count)
    ]
    while len(parts) > 1:
        parts = [jnp.maximum(parts[i], parts[i + 1]) for i in range(0, len(parts), 2)]
    return parts[0]


def local_slots(page_table, base, slot_count):
    request_count, page_count = page_table.shape
    flat = page_table.reshape(-1) - base
    valid = (flat >= 0) & (flat < slot_count)
    high = jnp.where(valid, flat // LOW_BLOCK, -1)
    low = flat % LOW_BLOCK
    entry = jnp.arange(request_count * page_count, dtype=jnp.int32)
    owner_code = (entry // page_count + 1).astype(jnp.float32)
    page_code = (entry % page_count).astype(jnp.float32)
    high_count = slot_count // LOW_BLOCK
    high_hot = (high[None, :] == jnp.arange(high_count, dtype=jnp.int32)[:, None]).astype(jnp.float32)
    low_hot = (low[None, :] == jnp.arange(LOW_BLOCK, dtype=jnp.int32)[:, None]).astype(jnp.bfloat16)
    coded = jnp.concatenate(
        [high_hot * owner_code[None, :], high_hot * page_code[None, :]], axis=0
    ).astype(jnp.bfloat16)
    table = lax.dot_general(
        coded, low_hot, (((1,), (1,)), ((), ())), preferred_element_type=jnp.float32
    )
    table = table.reshape(2, slot_count).astype(jnp.int32)
    owner = table[0] - 1
    page = table[1]
    return owner, page


def local_attention(queries, forget_log, kv_layer, decay_layer, owner, live, member):
    slots, tokens, heads, width = kv_layer.shape
    safe_owner = jnp.maximum(owner, 0)
    slot_queries = queries[safe_owner]
    padded = jnp.concatenate([slot_queries, jnp.zeros_like(slot_queries)], axis=2)
    diagonal = jnp.eye(heads, dtype=jnp.bfloat16)
    query_block = diagonal[None, :, :, None] * padded[:, :, None, :]
    scores = jnp.einsum(
        "pthc,pkhc->pkt", kv_layer, query_block, preferred_element_type=jnp.float32
    ) * SCORE_SCALE
    scores = scores + decay_layer + forget_log[safe_owner][:, :, None]
    scores = jnp.where(live[:, None, :], scores, NEGATIVE)
    page_peak = jnp.max(scores, axis=2)
    row_peak = jnp.max(jnp.where(member[:, :, None], page_peak[None], NEGATIVE), axis=1)
    slot_peak = row_peak[safe_owner]
    weights = jnp.where(live[:, None, :], jnp.exp(scores - slot_peak[:, :, None]), 0.0)
    page_sum = jnp.sum(weights, axis=2)
    mixed = jnp.einsum(
        "pkt,pthc->pkhc", weights.astype(jnp.bfloat16), kv_layer, preferred_element_type=jnp.float32
    )
    page_out = jnp.stack([mixed[:, h, h, HEAD:] for h in range(heads)], axis=1)
    member_f = member.astype(jnp.float32)
    row_sum = jnp.einsum("rp,ph->rh", member_f, page_sum, precision=lax.Precision.HIGHEST)
    row_out = jnp.einsum("rp,phd->rhd", member_f, page_out, precision=lax.Precision.HIGHEST)
    return row_peak, row_sum, row_out


def merge_pages(row_peak, row_sum, row_out):
    packed = jnp.concatenate([row_peak[:, :, None], row_sum[:, :, None], row_out], axis=2)
    count = lax.axis_size("gx")
    every = gather_all(packed, "gx")
    top = butterfly([part[:, :, 0] for part in every], jnp.maximum)
    scales = [jnp.exp(part[:, :, 0] - top) for part in every]
    total = butterfly([scale * part[:, :, 1] for scale, part in zip(scales, every)], jnp.add)
    out = butterfly(
        [scale[..., None] * part[:, :, 2:] for scale, part in zip(scales, every)], jnp.add
    )
    return top, total, out


def local(
    stream_in,
    attention_gain,
    feedforward_gain,
    final_gain,
    qkv_weight,
    forget_weight,
    forget_bias,
    out_weight,
    gate_weight,
    up_weight,
    down_weight,
    head_weight,
    kv_cache,
    decay_cache,
    lengths,
    page_table,
):
    local_pages = kv_cache.shape[1]
    local_heads = kv_cache.shape[3]
    request_count = stream_in.shape[0]
    width = stream_in.shape[1] * lax.axis_size("gx")
    base = lax.axis_index("gx") * local_pages
    owner, page = local_slots(page_table, base, local_pages)
    member = owner[None, :] == jnp.arange(request_count, dtype=jnp.int32)[:, None]
    slot_length = jnp.sum(jnp.where(member, lengths[:, None], 0), axis=0)
    offsets = jnp.arange(SHEET_ENTRIES, dtype=jnp.int32)
    live = (owner[:, None] >= 0) & (
        page[:, None] * SHEET_ENTRIES + offsets[None, :] < slot_length[:, None]
    )
    stream = stream_in.astype(jnp.float32)
    qkv_cols = qkv_weight.shape[2]
    for layer_id in range(DEPTH_NUMBER):
        squares = jnp.sum(stream * stream, axis=1)
        scaled = (stream * attention_gain[layer_id][None, :]).astype(jnp.bfloat16)
        qkv_part = jnp.dot(scaled, qkv_weight[layer_id], preferred_element_type=jnp.float32)
        forget_part = jnp.dot(scaled, forget_weight[layer_id], preferred_element_type=jnp.float32)
        total = xor_sum(
            jnp.concatenate(
                [qkv_part.astype(jnp.bfloat16), forget_part.astype(jnp.bfloat16), split_pair(squares)],
                axis=1,
            ),
            "gx",
            jnp.float32,
        )
        rms_value = jnp.sqrt((total[:, -2] + total[:, -1]) / width + EPSILON)
        projected = (total[:, :qkv_cols] / rms_value[:, None]).reshape(
            request_count, local_heads, 3 * HEAD
        )
        forget_logit = total[:, qkv_cols : qkv_cols + local_heads] / rms_value[:, None]
        queries = projected[:, :, :HEAD].astype(jnp.bfloat16)
        new_keys = projected[:, :, HEAD : 2 * HEAD].astype(jnp.bfloat16)
        new_values = projected[:, :, 2 * HEAD :].astype(jnp.bfloat16)
        forget_log = jax.nn.log_sigmoid(forget_logit + forget_bias[layer_id][None, :])
        local_peak, local_sum, local_out = local_attention(
            queries, forget_log, kv_cache[layer_id], decay_cache[layer_id], owner, live, member
        )
        row_peak, row_sum, row_out = merge_pages(local_peak, local_sum, local_out)
        own_score = (
            jnp.sum(queries.astype(jnp.float32) * new_keys.astype(jnp.float32), axis=2)
            * SCORE_SCALE
        )
        full_peak = jnp.maximum(row_peak, own_score)
        cache_scale = jnp.exp(row_peak - full_peak)
        own_weight = jnp.exp(own_score - full_peak)
        own_rounded = lax.optimization_barrier(own_weight.astype(jnp.bfloat16)).astype(jnp.float32)
        numerator = cache_scale[:, :, None] * row_out + own_rounded[:, :, None] * new_values.astype(
            jnp.float32
        )
        denominator = cache_scale * row_sum + own_weight
        attended = (
            (numerator / denominator[:, :, None])
            .reshape(request_count, local_heads * HEAD)
            .astype(jnp.bfloat16)
        )
        stream = stream + core_first_sum(
            jnp.dot(attended, out_weight[layer_id], preferred_element_type=jnp.float32), "gy"
        )
        squares = jnp.sum(stream * stream, axis=1)
        scaled = (stream * feedforward_gain[layer_id][None, :]).astype(jnp.bfloat16)
        gate_part = jnp.dot(scaled, gate_weight[layer_id], preferred_element_type=jnp.float32)
        up_part = jnp.dot(scaled, up_weight[layer_id], preferred_element_type=jnp.float32)
        hidden_cols = gate_part.shape[1]
        total = gather_sum(
            jnp.concatenate(
                [gate_part.astype(jnp.bfloat16), up_part.astype(jnp.bfloat16), split_pair(squares)],
                axis=1,
            ),
            "gx",
        )
        rms_value = jnp.sqrt((total[:, -2] + total[:, -1]) / width + EPSILON)
        gate_full = total[:, :hidden_cols] / rms_value[:, None]
        up_full = total[:, hidden_cols : 2 * hidden_cols] / rms_value[:, None]
        hidden = (jax.nn.silu(gate_full) * up_full).astype(jnp.bfloat16)
        stream = stream + core_first_sum(
            jnp.dot(hidden, down_weight[layer_id], preferred_element_type=jnp.float32), "gy"
        )
    squares = jnp.sum(stream * stream, axis=1)
    scaled = (stream * final_gain[None, :]).astype(jnp.bfloat16)
    logits = jnp.dot(scaled, head_weight, preferred_element_type=jnp.float32)
    parts = lax.axis_size("gx")
    chunk = logits.shape[1] // parts
    squares_pair = split_pair(squares)
    pieces = jnp.concatenate(
        [
            logits.astype(jnp.bfloat16).reshape(request_count, parts, chunk),
            jnp.broadcast_to(squares_pair[:, None, :], (request_count, parts, 2)),
        ],
        axis=2,
    )
    pieces = lax.all_to_all(pieces, "gx", 1, 1, tiled=True).astype(jnp.float32)
    top_part = jnp.sum(pieces[:, :, :chunk], axis=1)
    total_squares = jnp.sum(pieces[:, :, chunk] + pieces[:, :, chunk + 1], axis=1)
    rms_value = jnp.sqrt(total_squares / width + EPSILON)
    final_hidden = (stream / rms_value[:, None] * final_gain[None, :]).astype(jnp.bfloat16)
    local_top = jnp.max(top_part, axis=1) / rms_value
    top_logits = core_first_max(butterfly(gather_all(local_top, "gx"), jnp.maximum), "gy")
    return (final_hidden, rms_value, top_logits)


def solution(mesh):
    placed = (
        P(None, "gx"),
        P(None, "gx"),
        P(None, "gx"),
        P("gx"),
        P(None, "gx", "gy"),
        P(None, "gx", "gy"),
        P(None, "gy"),
        P(None, "gy", "gx"),
        P(None, "gx", "gy"),
        P(None, "gx", "gy"),
        P(None, "gy", "gx"),
        P("gx", "gy"),
        P(None, "gx", None, "gy", None),
        P(None, "gx", "gy", None),
        P(),
        P(),
    )
    return jax.shard_map(
        local, mesh=mesh, in_specs=placed, out_specs=(P(None, "gx"), P(), P()), check_vma=False
    )
```

```python
import jax
import jax.numpy as jnp
from jax import lax
from jax.sharding import PartitionSpec as P
from jax.experimental import pallas as pl
from jax.experimental.pallas import tpu as pltpu

HEAD = 64
DEPTH_NUMBER = 2
SHEET_ENTRIES = 128

SCORE_SCALE = 0.125
NEGATIVE = -1e30
EPSILON = 1e-06
LOW_BLOCK = 16


def gather_sum(value, axis):
    return jnp.sum(lax.all_gather(value, axis).astype(jnp.float32), axis=0)


def xor_sum(value, axis, kind=None):
    count = lax.axis_size(axis)
    parts = [value] + [
        lax.ppermute(value, axis, [(i, i ^ k) for i in range(count)]) for k in range(1, count)
    ]
    if kind is not None:
        parts = [part.astype(kind) for part in parts]
    while len(parts) > 1:
        parts = [parts[i] + parts[i + 1] for i in range(0, len(parts), 2)]
    return parts[0]


def butterfly(parts, join):
    while len(parts) > 1:
        parts = [join(parts[i], parts[i + 1]) for i in range(0, len(parts), 2)]
    return parts[0]


def exchange(value, axis, partner):
    count = lax.axis_size(axis)
    return lax.ppermute(value, axis, [(i, i ^ partner) for i in range(count)])


def core_first_sum(value, axis):
    carried = value.astype(jnp.bfloat16)
    pair = carried.astype(jnp.float32) + exchange(carried, axis, 1).astype(jnp.float32)
    pair = pair.astype(jnp.bfloat16)
    count = lax.axis_size(axis)
    parts = [pair] + [exchange(pair, axis, k) for k in range(2, count, 2)]
    return butterfly([part.astype(jnp.float32) for part in parts], jnp.add)


def core_first_max(value, axis):
    pair = jnp.maximum(value, exchange(value, axis, 1))
    count = lax.axis_size(axis)
    parts = [pair] + [exchange(pair, axis, k) for k in range(2, count, 2)]
    return butterfly(parts, jnp.maximum)


def split_pair(value):
    high = value.astype(jnp.bfloat16)
    low = (value - high.astype(jnp.float32)).astype(jnp.bfloat16)
    return jnp.stack([high, low], axis=1)


def xor_max(value, axis):
    count = lax.axis_size(axis)
    parts = [value] + [
        lax.ppermute(value, axis, [(i, i ^ k) for i in range(count)]) for k in range(1, count)
    ]
    while len(parts) > 1:
        parts = [jnp.maximum(parts[i], parts[i + 1]) for i in range(0, len(parts), 2)]
    return parts[0]


def copy_block(source, target):
    target[...] = source[...]


def layer_slice(cache, layer_id):
    layers, slots, tokens, heads, width = cache.shape
    block = 16
    return pl.pallas_call(
        copy_block,
        grid=(slots // block,),
        in_specs=[pl.BlockSpec((None, block, tokens, heads, width), lambda i: (layer_id, i, 0, 0, 0))],
        out_specs=pl.BlockSpec((block, tokens, heads, width), lambda i: (i, 0, 0, 0)),
        out_shape=jax.ShapeDtypeStruct((slots, tokens, heads, width), cache.dtype),
        cost_estimate=pl.CostEstimate(
            flops=0, transcendentals=0, bytes_accessed=2 * slots * tokens * heads * width * 2
        ),
    )(cache)


def local_slots(page_table, base, slot_count):
    request_count, page_count = page_table.shape
    flat = page_table.reshape(-1) - base
    valid = (flat >= 0) & (flat < slot_count)
    high = jnp.where(valid, flat // LOW_BLOCK, -1)
    low = flat % LOW_BLOCK
    entry = jnp.arange(request_count * page_count, dtype=jnp.int32)
    owner_code = (entry // page_count + 1).astype(jnp.float32)
    page_code = (entry % page_count).astype(jnp.float32)
    high_count = slot_count // LOW_BLOCK
    high_hot = (high[None, :] == jnp.arange(high_count, dtype=jnp.int32)[:, None]).astype(jnp.float32)
    low_hot = (low[None, :] == jnp.arange(LOW_BLOCK, dtype=jnp.int32)[:, None]).astype(jnp.bfloat16)
    coded = jnp.concatenate(
        [high_hot * owner_code[None, :], high_hot * page_code[None, :]], axis=0
    ).astype(jnp.bfloat16)
    table = lax.dot_general(
        coded, low_hot, (((1,), (1,)), ((), ())), preferred_element_type=jnp.float32
    )
    table = table.reshape(2, slot_count).astype(jnp.int32)
    owner = table[0] - 1
    page = table[1]
    return owner, page


def local_attention(queries, forget_log, kv_layer, decay_layer, owner, live, member):
    slots, tokens, heads, width = kv_layer.shape
    safe_owner = jnp.maximum(owner, 0)
    slot_queries = queries[safe_owner]
    padded = jnp.concatenate([slot_queries, jnp.zeros_like(slot_queries)], axis=2)
    diagonal = jnp.eye(heads, dtype=jnp.bfloat16)
    query_block = diagonal[None, :, :, None] * padded[:, :, None, :]
    scores = jnp.einsum(
        "pthc,pkhc->pkt", kv_layer, query_block, preferred_element_type=jnp.float32
    ) * SCORE_SCALE
    scores = scores + decay_layer + forget_log[safe_owner][:, :, None]
    scores = jnp.where(live[:, None, :], scores, NEGATIVE)
    page_peak = jnp.max(scores, axis=2)
    row_peak = jnp.max(jnp.where(member[:, :, None], page_peak[None], NEGATIVE), axis=1)
    slot_peak = row_peak[safe_owner]
    weights = jnp.where(live[:, None, :], jnp.exp(scores - slot_peak[:, :, None]), 0.0)
    page_sum = jnp.sum(weights, axis=2)
    mixed = jnp.einsum(
        "pkt,pthc->pkhc", weights.astype(jnp.bfloat16), kv_layer, preferred_element_type=jnp.float32
    )
    page_out = jnp.stack([mixed[:, h, h, HEAD:] for h in range(heads)], axis=1)
    member_f = member.astype(jnp.float32)
    row_sum = jnp.einsum("rp,ph->rh", member_f, page_sum, precision=lax.Precision.HIGHEST)
    row_out = jnp.einsum("rp,phd->rhd", member_f, page_out, precision=lax.Precision.HIGHEST)
    return row_peak, row_sum, row_out


def merge_pages(row_peak, row_sum, row_out):
    packed = jnp.concatenate([row_peak[:, :, None], row_sum[:, :, None], row_out], axis=2)
    count = lax.axis_size("gx")
    every = [packed] + [exchange(packed, "gx", k) for k in range(1, count)]
    top = butterfly([part[:, :, 0] for part in every], jnp.maximum)
    scales = [jnp.exp(part[:, :, 0] - top) for part in every]
    total = butterfly([scale * part[:, :, 1] for scale, part in zip(scales, every)], jnp.add)
    out = butterfly(
        [scale[..., None] * part[:, :, 2:] for scale, part in zip(scales, every)], jnp.add
    )
    return top, total, out


def local(
    stream_in,
    attention_gain,
    feedforward_gain,
    final_gain,
    qkv_weight,
    forget_weight,
    forget_bias,
    out_weight,
    gate_weight,
    up_weight,
    down_weight,
    head_weight,
    kv_cache,
    decay_cache,
    lengths,
    page_table,
):
    local_pages = kv_cache.shape[1]
    local_heads = kv_cache.shape[3]
    request_count = stream_in.shape[0]
    width = stream_in.shape[1] * lax.axis_size("gx")
    base = lax.axis_index("gx") * local_pages
    owner, page = local_slots(page_table, base, local_pages)
    member = owner[None, :] == jnp.arange(request_count, dtype=jnp.int32)[:, None]
    slot_length = jnp.sum(jnp.where(member, lengths[:, None], 0), axis=0)
    offsets = jnp.arange(SHEET_ENTRIES, dtype=jnp.int32)
    live = (owner[:, None] >= 0) & (
        page[:, None] * SHEET_ENTRIES + offsets[None, :] < slot_length[:, None]
    )
    stream = stream_in.astype(jnp.float32)
    qkv_cols = qkv_weight.shape[2]
    for layer_id in range(DEPTH_NUMBER):
        squares = jnp.sum(stream * stream, axis=1)
        scaled = (stream * attention_gain[layer_id][None, :]).astype(jnp.bfloat16)
        qkv_part = jnp.dot(scaled, qkv_weight[layer_id], preferred_element_type=jnp.float32)
        forget_part = jnp.dot(scaled, forget_weight[layer_id], preferred_element_type=jnp.float32)
        total = xor_sum(
            jnp.concatenate(
                [qkv_part.astype(jnp.bfloat16), forget_part.astype(jnp.bfloat16), split_pair(squares)],
                axis=1,
            ),
            "gx",
            jnp.float32,
        )
        rms_value = jnp.sqrt((total[:, -2] + total[:, -1]) / width + EPSILON)
        projected = (total[:, :qkv_cols] / rms_value[:, None]).reshape(
            request_count, local_heads, 3 * HEAD
        )
        forget_logit = total[:, qkv_cols : qkv_cols + local_heads] / rms_value[:, None]
        queries = projected[:, :, :HEAD].astype(jnp.bfloat16)
        new_keys = projected[:, :, HEAD : 2 * HEAD].astype(jnp.bfloat16)
        new_values = projected[:, :, 2 * HEAD :].astype(jnp.bfloat16)
        forget_log = jax.nn.log_sigmoid(forget_logit + forget_bias[layer_id][None, :])
        local_peak, local_sum, local_out = local_attention(
            queries, forget_log, layer_slice(kv_cache, layer_id), decay_cache[layer_id], owner, live, member
        )
        row_peak, row_sum, row_out = merge_pages(local_peak, local_sum, local_out)
        own_score = (
            jnp.sum(queries.astype(jnp.float32) * new_keys.astype(jnp.float32), axis=2)
            * SCORE_SCALE
        )
        full_peak = jnp.maximum(row_peak, own_score)
        cache_scale = jnp.exp(row_peak - full_peak)
        own_weight = jnp.exp(own_score - full_peak)
        own_rounded = lax.optimization_barrier(own_weight.astype(jnp.bfloat16)).astype(jnp.float32)
        numerator = cache_scale[:, :, None] * row_out + own_rounded[:, :, None] * new_values.astype(
            jnp.float32
        )
        denominator = cache_scale * row_sum + own_weight
        attended = (
            (numerator / denominator[:, :, None])
            .reshape(request_count, local_heads * HEAD)
            .astype(jnp.bfloat16)
        )
        stream = stream + core_first_sum(
            jnp.dot(attended, out_weight[layer_id], preferred_element_type=jnp.float32), "gy"
        )
        squares = jnp.sum(stream * stream, axis=1)
        scaled = (stream * feedforward_gain[layer_id][None, :]).astype(jnp.bfloat16)
        gate_part = jnp.dot(scaled, gate_weight[layer_id], preferred_element_type=jnp.float32)
        up_part = jnp.dot(scaled, up_weight[layer_id], preferred_element_type=jnp.float32)
        hidden_cols = gate_part.shape[1]
        total = gather_sum(
            jnp.concatenate(
                [gate_part.astype(jnp.bfloat16), up_part.astype(jnp.bfloat16), split_pair(squares)],
                axis=1,
            ),
            "gx",
        )
        rms_value = jnp.sqrt((total[:, -2] + total[:, -1]) / width + EPSILON)
        gate_full = total[:, :hidden_cols] / rms_value[:, None]
        up_full = total[:, hidden_cols : 2 * hidden_cols] / rms_value[:, None]
        hidden = (jax.nn.silu(gate_full) * up_full).astype(jnp.bfloat16)
        stream = stream + core_first_sum(
            jnp.dot(hidden, down_weight[layer_id], preferred_element_type=jnp.float32), "gy"
        )
    squares = jnp.sum(stream * stream, axis=1)
    scaled = (stream * final_gain[None, :]).astype(jnp.bfloat16)
    logits = jnp.dot(scaled, head_weight, preferred_element_type=jnp.float32)
    parts = lax.axis_size("gx")
    chunk = logits.shape[1] // parts
    squares_pair = split_pair(squares)
    pieces = jnp.concatenate(
        [
            logits.astype(jnp.bfloat16).reshape(request_count, parts, chunk),
            jnp.broadcast_to(squares_pair[:, None, :], (request_count, parts, 2)),
        ],
        axis=2,
    )
    pieces = lax.all_to_all(pieces, "gx", 1, 1, tiled=True).astype(jnp.float32)
    top_part = jnp.sum(pieces[:, :, :chunk], axis=1)
    total_squares = jnp.sum(pieces[:, :, chunk] + pieces[:, :, chunk + 1], axis=1)
    rms_value = jnp.sqrt(total_squares / width + EPSILON)
    final_hidden = (stream / rms_value[:, None] * final_gain[None, :]).astype(jnp.bfloat16)
    local_top = jnp.max(top_part, axis=1) / rms_value
    top_logits = core_first_max(xor_max(local_top, "gx"), "gy")
    return (final_hidden, rms_value, top_logits)


def solution(mesh):
    placed = (
        P(None, "gx"),
        P(None, "gx"),
        P(None, "gx"),
        P("gx"),
        P(None, "gx", "gy"),
        P(None, "gx", "gy"),
        P(None, "gy"),
        P(None, "gy", "gx"),
        P(None, "gx", "gy"),
        P(None, "gx", "gy"),
        P(None, "gy", "gx"),
        P("gx", "gy"),
        P(None, "gx", None, "gy", None),
        P(None, "gx", "gy", None),
        P(),
        P(),
    )
    return jax.shard_map(
        local, mesh=mesh, in_specs=placed, out_specs=(P(None, "gx"), P(), P()), check_vma=False
    )
```

```python
import jax
import jax.numpy as jnp
from jax import lax
from jax.sharding import PartitionSpec as P
from jax.experimental import pallas as pl
from jax.experimental.pallas import tpu as pltpu

HEAD = 64
DEPTH_NUMBER = 2
SHEET_ENTRIES = 128

SCORE_SCALE = 0.125
NEGATIVE = -1e30
EPSILON = 1e-06
LOW_BLOCK = 16


def gather_sum(value, axis):
    return jnp.sum(lax.all_gather(value, axis).astype(jnp.float32), axis=0)


def xor_sum(value, axis, kind=None):
    count = lax.axis_size(axis)
    parts = [value] + [
        lax.ppermute(value, axis, [(i, i ^ k) for i in range(count)]) for k in range(1, count)
    ]
    if kind is not None:
        parts = [part.astype(kind) for part in parts]
    while len(parts) > 1:
        parts = [parts[i] + parts[i + 1] for i in range(0, len(parts), 2)]
    return parts[0]


def butterfly(parts, join):
    while len(parts) > 1:
        parts = [join(parts[i], parts[i + 1]) for i in range(0, len(parts), 2)]
    return parts[0]


def exchange(value, axis, partner):
    count = lax.axis_size(axis)
    return lax.ppermute(value, axis, [(i, i ^ partner) for i in range(count)])


def core_first_sum(value, axis):
    carried = value.astype(jnp.bfloat16)
    pair = carried.astype(jnp.float32) + exchange(carried, axis, 1).astype(jnp.float32)
    pair = pair.astype(jnp.bfloat16)
    count = lax.axis_size(axis)
    parts = [pair] + [exchange(pair, axis, k) for k in range(2, count, 2)]
    return butterfly([part.astype(jnp.float32) for part in parts], jnp.add)


def core_first_max(value, axis):
    pair = jnp.maximum(value, exchange(value, axis, 1))
    count = lax.axis_size(axis)
    parts = [pair] + [exchange(pair, axis, k) for k in range(2, count, 2)]
    return butterfly(parts, jnp.maximum)


def split_pair(value):
    high = value.astype(jnp.bfloat16)
    low = (value - high.astype(jnp.float32)).astype(jnp.bfloat16)
    return jnp.stack([high, low], axis=1)


def xor_max(value, axis):
    count = lax.axis_size(axis)
    parts = [value] + [
        lax.ppermute(value, axis, [(i, i ^ k) for i in range(count)]) for k in range(1, count)
    ]
    while len(parts) > 1:
        parts = [jnp.maximum(parts[i], parts[i + 1]) for i in range(0, len(parts), 2)]
    return parts[0]


def copy_block(source, target):
    target[...] = source[...]


def layer_slice(cache, layer_id):
    layers, slots, tokens, heads, width = cache.shape
    block = 32
    return pl.pallas_call(
        copy_block,
        grid=(slots // block,),
        in_specs=[pl.BlockSpec((None, block, tokens, heads, width), lambda i: (layer_id, i, 0, 0, 0))],
        out_specs=pl.BlockSpec((block, tokens, heads, width), lambda i: (i, 0, 0, 0)),
        out_shape=jax.ShapeDtypeStruct((slots, tokens, heads, width), cache.dtype),
        cost_estimate=pl.CostEstimate(
            flops=0, transcendentals=0, bytes_accessed=2 * slots * tokens * heads * width * 2
        ),
    )(cache)


def local_slots(page_table, base, slot_count):
    request_count, page_count = page_table.shape
    flat = page_table.reshape(-1) - base
    valid = (flat >= 0) & (flat < slot_count)
    high = jnp.where(valid, flat // LOW_BLOCK, -1)
    low = flat % LOW_BLOCK
    entry = jnp.arange(request_count * page_count, dtype=jnp.int32)
    owner_code = (entry // page_count + 1).astype(jnp.float32)
    page_code = (entry % page_count).astype(jnp.float32)
    high_count = slot_count // LOW_BLOCK
    high_hot = (high[None, :] == jnp.arange(high_count, dtype=jnp.int32)[:, None]).astype(jnp.float32)
    low_hot = (low[None, :] == jnp.arange(LOW_BLOCK, dtype=jnp.int32)[:, None]).astype(jnp.bfloat16)
    coded = jnp.concatenate(
        [high_hot * owner_code[None, :], high_hot * page_code[None, :]], axis=0
    ).astype(jnp.bfloat16)
    table = lax.dot_general(
        coded, low_hot, (((1,), (1,)), ((), ())), preferred_element_type=jnp.float32
    )
    table = table.reshape(2, slot_count).astype(jnp.int32)
    owner = table[0] - 1
    page = table[1]
    return owner, page


def local_attention(queries, forget_log, kv_layer, decay_layer, owner, live, member):
    slots, tokens, heads, width = kv_layer.shape
    safe_owner = jnp.maximum(owner, 0)
    slot_queries = queries[safe_owner]
    padded = jnp.concatenate([slot_queries, jnp.zeros_like(slot_queries)], axis=2)
    diagonal = jnp.eye(heads, dtype=jnp.bfloat16)
    query_block = diagonal[None, :, :, None] * padded[:, :, None, :]
    scores = jnp.einsum(
        "pthc,pkhc->pkt", kv_layer, query_block, preferred_element_type=jnp.float32
    ) * SCORE_SCALE
    scores = scores + decay_layer + forget_log[safe_owner][:, :, None]
    scores = jnp.where(live[:, None, :], scores, NEGATIVE)
    page_peak = jnp.max(scores, axis=2)
    row_peak = jnp.max(jnp.where(member[:, :, None], page_peak[None], NEGATIVE), axis=1)
    slot_peak = row_peak[safe_owner]
    weights = jnp.where(live[:, None, :], jnp.exp(scores - slot_peak[:, :, None]), 0.0)
    page_sum = jnp.sum(weights, axis=2)
    mixed = jnp.einsum(
        "pkt,pthc->pkhc", weights.astype(jnp.bfloat16), kv_layer, preferred_element_type=jnp.float32
    )
    page_out = jnp.stack([mixed[:, h, h, HEAD:] for h in range(heads)], axis=1)
    member_f = member.astype(jnp.float32)
    row_sum = jnp.einsum("rp,ph->rh", member_f, page_sum, precision=lax.Precision.HIGHEST)
    row_out = jnp.einsum("rp,phd->rhd", member_f, page_out, precision=lax.Precision.HIGHEST)
    return row_peak, row_sum, row_out


def merge_pages(row_peak, row_sum, row_out):
    packed = jnp.concatenate([row_peak[:, :, None], row_sum[:, :, None], row_out], axis=2)
    count = lax.axis_size("gx")
    every = [packed] + [exchange(packed, "gx", k) for k in range(1, count)]
    top = butterfly([part[:, :, 0] for part in every], jnp.maximum)
    scales = [jnp.exp(part[:, :, 0] - top) for part in every]
    total = butterfly([scale * part[:, :, 1] for scale, part in zip(scales, every)], jnp.add)
    out = butterfly(
        [scale[..., None] * part[:, :, 2:] for scale, part in zip(scales, every)], jnp.add
    )
    return top, total, out


def local(
    stream_in,
    attention_gain,
    feedforward_gain,
    final_gain,
    qkv_weight,
    forget_weight,
    forget_bias,
    out_weight,
    gate_weight,
    up_weight,
    down_weight,
    head_weight,
    kv_cache,
    decay_cache,
    lengths,
    page_table,
):
    local_pages = kv_cache.shape[1]
    local_heads = kv_cache.shape[3]
    request_count = stream_in.shape[0]
    width = stream_in.shape[1] * lax.axis_size("gx")
    base = lax.axis_index("gx") * local_pages
    owner, page = local_slots(page_table, base, local_pages)
    member = owner[None, :] == jnp.arange(request_count, dtype=jnp.int32)[:, None]
    slot_length = jnp.sum(jnp.where(member, lengths[:, None], 0), axis=0)
    offsets = jnp.arange(SHEET_ENTRIES, dtype=jnp.int32)
    live = (owner[:, None] >= 0) & (
        page[:, None] * SHEET_ENTRIES + offsets[None, :] < slot_length[:, None]
    )
    stream = stream_in.astype(jnp.float32)
    qkv_cols = qkv_weight.shape[2]
    for layer_id in range(DEPTH_NUMBER):
        squares = jnp.sum(stream * stream, axis=1)
        scaled = (stream * attention_gain[layer_id][None, :]).astype(jnp.bfloat16)
        qkv_part = jnp.dot(scaled, qkv_weight[layer_id], preferred_element_type=jnp.float32)
        forget_part = jnp.dot(scaled, forget_weight[layer_id], preferred_element_type=jnp.float32)
        total = xor_sum(
            jnp.concatenate(
                [qkv_part.astype(jnp.bfloat16), forget_part.astype(jnp.bfloat16), split_pair(squares)],
                axis=1,
            ),
            "gx",
            jnp.float32,
        )
        rms_value = jnp.sqrt((total[:, -2] + total[:, -1]) / width + EPSILON)
        projected = (total[:, :qkv_cols] / rms_value[:, None]).reshape(
            request_count, local_heads, 3 * HEAD
        )
        forget_logit = total[:, qkv_cols : qkv_cols + local_heads] / rms_value[:, None]
        queries = projected[:, :, :HEAD].astype(jnp.bfloat16)
        new_keys = projected[:, :, HEAD : 2 * HEAD].astype(jnp.bfloat16)
        new_values = projected[:, :, 2 * HEAD :].astype(jnp.bfloat16)
        forget_log = jax.nn.log_sigmoid(forget_logit + forget_bias[layer_id][None, :])
        local_peak, local_sum, local_out = local_attention(
            queries, forget_log, layer_slice(kv_cache, layer_id), decay_cache[layer_id], owner, live, member
        )
        row_peak, row_sum, row_out = merge_pages(local_peak, local_sum, local_out)
        own_score = (
            jnp.sum(queries.astype(jnp.float32) * new_keys.astype(jnp.float32), axis=2)
            * SCORE_SCALE
        )
        full_peak = jnp.maximum(row_peak, own_score)
        cache_scale = jnp.exp(row_peak - full_peak)
        own_weight = jnp.exp(own_score - full_peak)
        own_rounded = lax.optimization_barrier(own_weight.astype(jnp.bfloat16)).astype(jnp.float32)
        numerator = cache_scale[:, :, None] * row_out + own_rounded[:, :, None] * new_values.astype(
            jnp.float32
        )
        denominator = cache_scale * row_sum + own_weight
        attended = (
            (numerator / denominator[:, :, None])
            .reshape(request_count, local_heads * HEAD)
            .astype(jnp.bfloat16)
        )
        stream = stream + core_first_sum(
            jnp.dot(attended, out_weight[layer_id], preferred_element_type=jnp.float32), "gy"
        )
        squares = jnp.sum(stream * stream, axis=1)
        scaled = (stream * feedforward_gain[layer_id][None, :]).astype(jnp.bfloat16)
        gate_part = jnp.dot(scaled, gate_weight[layer_id], preferred_element_type=jnp.float32)
        up_part = jnp.dot(scaled, up_weight[layer_id], preferred_element_type=jnp.float32)
        hidden_cols = gate_part.shape[1]
        total = gather_sum(
            jnp.concatenate(
                [gate_part.astype(jnp.bfloat16), up_part.astype(jnp.bfloat16), split_pair(squares)],
                axis=1,
            ),
            "gx",
        )
        rms_value = jnp.sqrt((total[:, -2] + total[:, -1]) / width + EPSILON)
        gate_full = total[:, :hidden_cols] / rms_value[:, None]
        up_full = total[:, hidden_cols : 2 * hidden_cols] / rms_value[:, None]
        hidden = (jax.nn.silu(gate_full) * up_full).astype(jnp.bfloat16)
        stream = stream + core_first_sum(
            jnp.dot(hidden, down_weight[layer_id], preferred_element_type=jnp.float32), "gy"
        )
    squares = jnp.sum(stream * stream, axis=1)
    scaled = (stream * final_gain[None, :]).astype(jnp.bfloat16)
    logits = jnp.dot(scaled, head_weight, preferred_element_type=jnp.float32)
    parts = lax.axis_size("gx")
    chunk = logits.shape[1] // parts
    squares_pair = split_pair(squares)
    pieces = jnp.concatenate(
        [
            logits.astype(jnp.bfloat16).reshape(request_count, parts, chunk),
            jnp.broadcast_to(squares_pair[:, None, :], (request_count, parts, 2)),
        ],
        axis=2,
    )
    pieces = lax.all_to_all(pieces, "gx", 1, 1, tiled=True).astype(jnp.float32)
    top_part = jnp.sum(pieces[:, :, :chunk], axis=1)
    total_squares = jnp.sum(pieces[:, :, chunk] + pieces[:, :, chunk + 1], axis=1)
    rms_value = jnp.sqrt(total_squares / width + EPSILON)
    final_hidden = (stream / rms_value[:, None] * final_gain[None, :]).astype(jnp.bfloat16)
    local_top = jnp.max(top_part, axis=1) / rms_value
    top_logits = core_first_max(xor_max(local_top, "gx"), "gy")
    return (final_hidden, rms_value, top_logits)


def solution(mesh):
    placed = (
        P(None, "gx"),
        P(None, "gx"),
        P(None, "gx"),
        P("gx"),
        P(None, "gx", "gy"),
        P(None, "gx", "gy"),
        P(None, "gy"),
        P(None, "gy", "gx"),
        P(None, "gx", "gy"),
        P(None, "gx", "gy"),
        P(None, "gy", "gx"),
        P("gx", "gy"),
        P(None, "gx", None, "gy", None),
        P(None, "gx", "gy", None),
        P(),
        P(),
    )
    return jax.shard_map(
        local, mesh=mesh, in_specs=placed, out_specs=(P(None, "gx"), P(), P()), check_vma=False
    )
```

```python
import jax
import jax.numpy as jnp
from jax import lax
from jax.sharding import PartitionSpec as P
from jax.experimental import pallas as pl
from jax.experimental.pallas import tpu as pltpu

HEAD = 64
DEPTH_NUMBER = 2
SHEET_ENTRIES = 128

SCORE_SCALE = 0.125
NEGATIVE = -1e30
EPSILON = 1e-06
LOW_BLOCK = 16


def gather_sum(value, axis):
    return jnp.sum(lax.all_gather(value, axis).astype(jnp.float32), axis=0)


def xor_sum(value, axis, kind=None):
    count = lax.axis_size(axis)
    parts = [value] + [
        lax.ppermute(value, axis, [(i, i ^ k) for i in range(count)]) for k in range(1, count)
    ]
    if kind is not None:
        parts = [part.astype(kind) for part in parts]
    while len(parts) > 1:
        parts = [parts[i] + parts[i + 1] for i in range(0, len(parts), 2)]
    return parts[0]


def butterfly(parts, join):
    while len(parts) > 1:
        parts = [join(parts[i], parts[i + 1]) for i in range(0, len(parts), 2)]
    return parts[0]


def exchange(value, axis, partner):
    count = lax.axis_size(axis)
    return lax.ppermute(value, axis, [(i, i ^ partner) for i in range(count)])


def core_first_sum(value, axis):
    carried = value.astype(jnp.bfloat16)
    pair = carried.astype(jnp.float32) + exchange(carried, axis, 1).astype(jnp.float32)
    pair = pair.astype(jnp.bfloat16)
    count = lax.axis_size(axis)
    parts = [pair] + [exchange(pair, axis, k) for k in range(2, count, 2)]
    return butterfly([part.astype(jnp.float32) for part in parts], jnp.add)


def core_first_max(value, axis):
    pair = jnp.maximum(value, exchange(value, axis, 1))
    count = lax.axis_size(axis)
    parts = [pair] + [exchange(pair, axis, k) for k in range(2, count, 2)]
    return butterfly(parts, jnp.maximum)


def split_pair(value):
    high = value.astype(jnp.bfloat16)
    low = (value - high.astype(jnp.float32)).astype(jnp.bfloat16)
    return jnp.stack([high, low], axis=1)


def xor_max(value, axis):
    count = lax.axis_size(axis)
    parts = [value] + [
        lax.ppermute(value, axis, [(i, i ^ k) for i in range(count)]) for k in range(1, count)
    ]
    while len(parts) > 1:
        parts = [jnp.maximum(parts[i], parts[i + 1]) for i in range(0, len(parts), 2)]
    return parts[0]


def copy_block(source, target):
    target[...] = source[...]


def layer_slice(cache, layer_id):
    layers, slots, tokens, heads, width = cache.shape
    block = 64
    return pl.pallas_call(
        copy_block,
        grid=(slots // block,),
        in_specs=[pl.BlockSpec((None, block, tokens, heads, width), lambda i: (layer_id, i, 0, 0, 0))],
        out_specs=pl.BlockSpec((block, tokens, heads, width), lambda i: (i, 0, 0, 0)),
        out_shape=jax.ShapeDtypeStruct((slots, tokens, heads, width), cache.dtype),
        cost_estimate=pl.CostEstimate(
            flops=0, transcendentals=0, bytes_accessed=2 * slots * tokens * heads * width * 2
        ),
    )(cache)


def local_slots(page_table, base, slot_count):
    request_count, page_count = page_table.shape
    flat = page_table.reshape(-1) - base
    valid = (flat >= 0) & (flat < slot_count)
    high = jnp.where(valid, flat // LOW_BLOCK, -1)
    low = flat % LOW_BLOCK
    entry = jnp.arange(request_count * page_count, dtype=jnp.int32)
    owner_code = (entry // page_count + 1).astype(jnp.float32)
    page_code = (entry % page_count).astype(jnp.float32)
    high_count = slot_count // LOW_BLOCK
    high_hot = (high[None, :] == jnp.arange(high_count, dtype=jnp.int32)[:, None]).astype(jnp.float32)
    low_hot = (low[None, :] == jnp.arange(LOW_BLOCK, dtype=jnp.int32)[:, None]).astype(jnp.bfloat16)
    coded = jnp.concatenate(
        [high_hot * owner_code[None, :], high_hot * page_code[None, :]], axis=0
    ).astype(jnp.bfloat16)
    table = lax.dot_general(
        coded, low_hot, (((1,), (1,)), ((), ())), preferred_element_type=jnp.float32
    )
    table = table.reshape(2, slot_count).astype(jnp.int32)
    owner = table[0] - 1
    page = table[1]
    return owner, page


def local_attention(queries, forget_log, kv_layer, decay_layer, owner, live, member):
    slots, tokens, heads, width = kv_layer.shape
    safe_owner = jnp.maximum(owner, 0)
    slot_queries = queries[safe_owner]
    padded = jnp.concatenate([slot_queries, jnp.zeros_like(slot_queries)], axis=2)
    diagonal = jnp.eye(heads, dtype=jnp.bfloat16)
    query_block = diagonal[None, :, :, None] * padded[:, :, None, :]
    scores = jnp.einsum(
        "pthc,pkhc->pkt", kv_layer, query_block, preferred_element_type=jnp.float32
    ) * SCORE_SCALE
    scores = scores + decay_layer + forget_log[safe_owner][:, :, None]
    scores = jnp.where(live[:, None, :], scores, NEGATIVE)
    page_peak = jnp.max(scores, axis=2)
    row_peak = jnp.max(jnp.where(member[:, :, None], page_peak[None], NEGATIVE), axis=1)
    slot_peak = row_peak[safe_owner]
    weights = jnp.where(live[:, None, :], jnp.exp(scores - slot_peak[:, :, None]), 0.0)
    page_sum = jnp.sum(weights, axis=2)
    mixed = jnp.einsum(
        "pkt,pthc->pkhc", weights.astype(jnp.bfloat16), kv_layer, preferred_element_type=jnp.float32
    )
    page_out = jnp.stack([mixed[:, h, h, HEAD:] for h in range(heads)], axis=1)
    member_f = member.astype(jnp.float32)
    row_sum = jnp.einsum("rp,ph->rh", member_f, page_sum, precision=lax.Precision.HIGHEST)
    row_out = jnp.einsum("rp,phd->rhd", member_f, page_out, precision=lax.Precision.HIGHEST)
    return row_peak, row_sum, row_out


def merge_pages(row_peak, row_sum, row_out):
    packed = jnp.concatenate([row_peak[:, :, None], row_sum[:, :, None], row_out], axis=2)
    count = lax.axis_size("gx")
    every = [packed] + [exchange(packed, "gx", k) for k in range(1, count)]
    top = butterfly([part[:, :, 0] for part in every], jnp.maximum)
    scales = [jnp.exp(part[:, :, 0] - top) for part in every]
    total = butterfly([scale * part[:, :, 1] for scale, part in zip(scales, every)], jnp.add)
    out = butterfly(
        [scale[..., None] * part[:, :, 2:] for scale, part in zip(scales, every)], jnp.add
    )
    return top, total, out


def local(
    stream_in,
    attention_gain,
    feedforward_gain,
    final_gain,
    qkv_weight,
    forget_weight,
    forget_bias,
    out_weight,
    gate_weight,
    up_weight,
    down_weight,
    head_weight,
    kv_cache,
    decay_cache,
    lengths,
    page_table,
):
    local_pages = kv_cache.shape[1]
    local_heads = kv_cache.shape[3]
    request_count = stream_in.shape[0]
    width = stream_in.shape[1] * lax.axis_size("gx")
    base = lax.axis_index("gx") * local_pages
    owner, page = local_slots(page_table, base, local_pages)
    member = owner[None, :] == jnp.arange(request_count, dtype=jnp.int32)[:, None]
    slot_length = jnp.sum(jnp.where(member, lengths[:, None], 0), axis=0)
    offsets = jnp.arange(SHEET_ENTRIES, dtype=jnp.int32)
    live = (owner[:, None] >= 0) & (
        page[:, None] * SHEET_ENTRIES + offsets[None, :] < slot_length[:, None]
    )
    stream = stream_in.astype(jnp.float32)
    qkv_cols = qkv_weight.shape[2]
    for layer_id in range(DEPTH_NUMBER):
        squares = jnp.sum(stream * stream, axis=1)
        scaled = (stream * attention_gain[layer_id][None, :]).astype(jnp.bfloat16)
        qkv_part = jnp.dot(scaled, qkv_weight[layer_id], preferred_element_type=jnp.float32)
        forget_part = jnp.dot(scaled, forget_weight[layer_id], preferred_element_type=jnp.float32)
        total = xor_sum(
            jnp.concatenate(
                [qkv_part.astype(jnp.bfloat16), forget_part.astype(jnp.bfloat16), split_pair(squares)],
                axis=1,
            ),
            "gx",
            jnp.float32,
        )
        rms_value = jnp.sqrt((total[:, -2] + total[:, -1]) / width + EPSILON)
        projected = (total[:, :qkv_cols] / rms_value[:, None]).reshape(
            request_count, local_heads, 3 * HEAD
        )
        forget_logit = total[:, qkv_cols : qkv_cols + local_heads] / rms_value[:, None]
        queries = projected[:, :, :HEAD].astype(jnp.bfloat16)
        new_keys = projected[:, :, HEAD : 2 * HEAD].astype(jnp.bfloat16)
        new_values = projected[:, :, 2 * HEAD :].astype(jnp.bfloat16)
        forget_log = jax.nn.log_sigmoid(forget_logit + forget_bias[layer_id][None, :])
        local_peak, local_sum, local_out = local_attention(
            queries, forget_log, layer_slice(kv_cache, layer_id), decay_cache[layer_id], owner, live, member
        )
        row_peak, row_sum, row_out = merge_pages(local_peak, local_sum, local_out)
        own_score = (
            jnp.sum(queries.astype(jnp.float32) * new_keys.astype(jnp.float32), axis=2)
            * SCORE_SCALE
        )
        full_peak = jnp.maximum(row_peak, own_score)
        cache_scale = jnp.exp(row_peak - full_peak)
        own_weight = jnp.exp(own_score - full_peak)
        own_rounded = lax.optimization_barrier(own_weight.astype(jnp.bfloat16)).astype(jnp.float32)
        numerator = cache_scale[:, :, None] * row_out + own_rounded[:, :, None] * new_values.astype(
            jnp.float32
        )
        denominator = cache_scale * row_sum + own_weight
        attended = (
            (numerator / denominator[:, :, None])
            .reshape(request_count, local_heads * HEAD)
            .astype(jnp.bfloat16)
        )
        stream = stream + core_first_sum(
            jnp.dot(attended, out_weight[layer_id], preferred_element_type=jnp.float32), "gy"
        )
        squares = jnp.sum(stream * stream, axis=1)
        scaled = (stream * feedforward_gain[layer_id][None, :]).astype(jnp.bfloat16)
        gate_part = jnp.dot(scaled, gate_weight[layer_id], preferred_element_type=jnp.float32)
        up_part = jnp.dot(scaled, up_weight[layer_id], preferred_element_type=jnp.float32)
        hidden_cols = gate_part.shape[1]
        total = gather_sum(
            jnp.concatenate(
                [gate_part.astype(jnp.bfloat16), up_part.astype(jnp.bfloat16), split_pair(squares)],
                axis=1,
            ),
            "gx",
        )
        rms_value = jnp.sqrt((total[:, -2] + total[:, -1]) / width + EPSILON)
        gate_full = total[:, :hidden_cols] / rms_value[:, None]
        up_full = total[:, hidden_cols : 2 * hidden_cols] / rms_value[:, None]
        hidden = (jax.nn.silu(gate_full) * up_full).astype(jnp.bfloat16)
        stream = stream + core_first_sum(
            jnp.dot(hidden, down_weight[layer_id], preferred_element_type=jnp.float32), "gy"
        )
    squares = jnp.sum(stream * stream, axis=1)
    scaled = (stream * final_gain[None, :]).astype(jnp.bfloat16)
    logits = jnp.dot(scaled, head_weight, preferred_element_type=jnp.float32)
    parts = lax.axis_size("gx")
    chunk = logits.shape[1] // parts
    squares_pair = split_pair(squares)
    pieces = jnp.concatenate(
        [
            logits.astype(jnp.bfloat16).reshape(request_count, parts, chunk),
            jnp.broadcast_to(squares_pair[:, None, :], (request_count, parts, 2)),
        ],
        axis=2,
    )
    pieces = lax.all_to_all(pieces, "gx", 1, 1, tiled=True).astype(jnp.float32)
    top_part = jnp.sum(pieces[:, :, :chunk], axis=1)
    total_squares = jnp.sum(pieces[:, :, chunk] + pieces[:, :, chunk + 1], axis=1)
    rms_value = jnp.sqrt(total_squares / width + EPSILON)
    final_hidden = (stream / rms_value[:, None] * final_gain[None, :]).astype(jnp.bfloat16)
    local_top = jnp.max(top_part, axis=1) / rms_value
    top_logits = core_first_max(xor_max(local_top, "gx"), "gy")
    return (final_hidden, rms_value, top_logits)


def solution(mesh):
    placed = (
        P(None, "gx"),
        P(None, "gx"),
        P(None, "gx"),
        P("gx"),
        P(None, "gx", "gy"),
        P(None, "gx", "gy"),
        P(None, "gy"),
        P(None, "gy", "gx"),
        P(None, "gx", "gy"),
        P(None, "gx", "gy"),
        P(None, "gy", "gx"),
        P("gx", "gy"),
        P(None, "gx", None, "gy", None),
        P(None, "gx", "gy", None),
        P(),
        P(),
    )
    return jax.shard_map(
        local, mesh=mesh, in_specs=placed, out_specs=(P(None, "gx"), P(), P()), check_vma=False
    )
```

```python
import jax
import jax.numpy as jnp
from jax import lax
from jax.sharding import PartitionSpec as P
from jax.experimental import pallas as pl
from jax.experimental.pallas import tpu as pltpu

HEAD = 64
DEPTH_NUMBER = 2
SHEET_ENTRIES = 128

SCORE_SCALE = 0.125
NEGATIVE = -1e30
EPSILON = 1e-06
LOW_BLOCK = 16


def gather_sum(value, axis):
    return jnp.sum(lax.all_gather(value, axis).astype(jnp.float32), axis=0)


def xor_sum(value, axis, kind=None):
    count = lax.axis_size(axis)
    parts = [value] + [
        lax.ppermute(value, axis, [(i, i ^ k) for i in range(count)]) for k in range(1, count)
    ]
    if kind is not None:
        parts = [part.astype(kind) for part in parts]
    while len(parts) > 1:
        parts = [parts[i] + parts[i + 1] for i in range(0, len(parts), 2)]
    return parts[0]


def butterfly(parts, join):
    while len(parts) > 1:
        parts = [join(parts[i], parts[i + 1]) for i in range(0, len(parts), 2)]
    return parts[0]


def exchange(value, axis, partner):
    count = lax.axis_size(axis)
    return lax.ppermute(value, axis, [(i, i ^ partner) for i in range(count)])


def core_first_sum(value, axis):
    carried = value.astype(jnp.bfloat16)
    pair = carried.astype(jnp.float32) + exchange(carried, axis, 1).astype(jnp.float32)
    pair = pair.astype(jnp.bfloat16)
    count = lax.axis_size(axis)
    parts = [pair] + [exchange(pair, axis, k) for k in range(2, count, 2)]
    return butterfly([part.astype(jnp.float32) for part in parts], jnp.add)


def core_first_max(value, axis):
    pair = jnp.maximum(value, exchange(value, axis, 1))
    count = lax.axis_size(axis)
    parts = [pair] + [exchange(pair, axis, k) for k in range(2, count, 2)]
    return butterfly(parts, jnp.maximum)


def split_pair(value):
    high = value.astype(jnp.bfloat16)
    low = (value - high.astype(jnp.float32)).astype(jnp.bfloat16)
    return jnp.stack([high, low], axis=1)


def xor_max(value, axis):
    count = lax.axis_size(axis)
    parts = [value] + [
        lax.ppermute(value, axis, [(i, i ^ k) for i in range(count)]) for k in range(1, count)
    ]
    while len(parts) > 1:
        parts = [jnp.maximum(parts[i], parts[i + 1]) for i in range(0, len(parts), 2)]
    return parts[0]


def copy_block(source, target):
    target[...] = source[...]


def layer_slice(cache, layer_id):
    layers, slots, tokens, heads, width = cache.shape
    block = 64
    return pl.pallas_call(
        copy_block,
        grid=(slots // block,),
        in_specs=[pl.BlockSpec((None, block, tokens, heads, width), lambda i: (layer_id, i, 0, 0, 0))],
        out_specs=pl.BlockSpec((block, tokens, heads, width), lambda i: (i, 0, 0, 0)),
        out_shape=jax.ShapeDtypeStruct((slots, tokens, heads, width), cache.dtype),
        cost_estimate=pl.CostEstimate(
            flops=0, transcendentals=0, bytes_accessed=2 * slots * tokens * heads * width * 2
        ),
    )(cache)


def local_slots(page_table, base, slot_count):
    request_count, page_count = page_table.shape
    flat = page_table.reshape(-1) - base
    valid = (flat >= 0) & (flat < slot_count)
    high = jnp.where(valid, flat // LOW_BLOCK, -1)
    low = flat % LOW_BLOCK
    entry = jnp.arange(request_count * page_count, dtype=jnp.int32)
    owner_code = (entry // page_count + 1).astype(jnp.float32)
    page_code = (entry % page_count).astype(jnp.float32)
    high_count = slot_count // LOW_BLOCK
    high_hot = (high[None, :] == jnp.arange(high_count, dtype=jnp.int32)[:, None]).astype(jnp.float32)
    low_hot = (low[None, :] == jnp.arange(LOW_BLOCK, dtype=jnp.int32)[:, None]).astype(jnp.bfloat16)
    coded = jnp.concatenate(
        [high_hot * owner_code[None, :], high_hot * page_code[None, :]], axis=0
    ).astype(jnp.bfloat16)
    table = lax.dot_general(
        coded, low_hot, (((1,), (1,)), ((), ())), preferred_element_type=jnp.float32
    )
    table = table.reshape(2, slot_count).astype(jnp.int32)
    owner = table[0] - 1
    page = table[1]
    return owner, page


def local_attention(queries, forget_log, kv_layer, decay_layer, owner, live, member):
    slots, tokens, heads, width = kv_layer.shape
    safe_owner = jnp.maximum(owner, 0)
    hot = member.T
    hot_half = hot.astype(jnp.bfloat16)
    hot_full = hot.astype(jnp.float32)
    slot_queries = jnp.einsum(
        "pr,rhd->phd", hot_half, queries, preferred_element_type=jnp.float32
    ).astype(jnp.bfloat16)
    padded = jnp.concatenate([slot_queries, jnp.zeros_like(slot_queries)], axis=2)
    diagonal = jnp.eye(heads, dtype=jnp.bfloat16)
    query_block = diagonal[None, :, :, None] * padded[:, :, None, :]
    scores = jnp.einsum(
        "pthc,pkhc->pkt", kv_layer, query_block, preferred_element_type=jnp.float32
    ) * SCORE_SCALE
    slot_forget = jnp.einsum("pr,rh->ph", hot_full, forget_log, precision=lax.Precision.HIGHEST)
    scores = scores + decay_layer + slot_forget[:, :, None]
    scores = jnp.where(live[:, None, :], scores, NEGATIVE)
    page_peak = jnp.max(scores, axis=2)
    row_peak = jnp.max(jnp.where(member[:, :, None], page_peak[None], NEGATIVE), axis=1)
    slot_peak = jnp.einsum("pr,rh->ph", hot_full, row_peak, precision=lax.Precision.HIGHEST)
    weights = jnp.where(live[:, None, :], jnp.exp(scores - slot_peak[:, :, None]), 0.0)
    page_sum = jnp.sum(weights, axis=2)
    mixed = jnp.einsum(
        "pkt,pthc->pkhc", weights.astype(jnp.bfloat16), kv_layer, preferred_element_type=jnp.float32
    )
    page_out = jnp.stack([mixed[:, h, h, HEAD:] for h in range(heads)], axis=1)
    member_f = member.astype(jnp.float32)
    row_sum = jnp.einsum("rp,ph->rh", member_f, page_sum, precision=lax.Precision.HIGHEST)
    row_out = jnp.einsum("rp,phd->rhd", member_f, page_out, precision=lax.Precision.HIGHEST)
    return row_peak, row_sum, row_out


def merge_pages(row_peak, row_sum, row_out):
    packed = jnp.concatenate([row_peak[:, :, None], row_sum[:, :, None], row_out], axis=2)
    count = lax.axis_size("gx")
    every = [packed] + [exchange(packed, "gx", k) for k in range(1, count)]
    top = butterfly([part[:, :, 0] for part in every], jnp.maximum)
    scales = [jnp.exp(part[:, :, 0] - top) for part in every]
    total = butterfly([scale * part[:, :, 1] for scale, part in zip(scales, every)], jnp.add)
    out = butterfly(
        [scale[..., None] * part[:, :, 2:] for scale, part in zip(scales, every)], jnp.add
    )
    return top, total, out


def local(
    stream_in,
    attention_gain,
    feedforward_gain,
    final_gain,
    qkv_weight,
    forget_weight,
    forget_bias,
    out_weight,
    gate_weight,
    up_weight,
    down_weight,
    head_weight,
    kv_cache,
    decay_cache,
    lengths,
    page_table,
):
    local_pages = kv_cache.shape[1]
    local_heads = kv_cache.shape[3]
    request_count = stream_in.shape[0]
    width = stream_in.shape[1] * lax.axis_size("gx")
    base = lax.axis_index("gx") * local_pages
    owner, page = local_slots(page_table, base, local_pages)
    member = owner[None, :] == jnp.arange(request_count, dtype=jnp.int32)[:, None]
    slot_length = jnp.sum(jnp.where(member, lengths[:, None], 0), axis=0)
    offsets = jnp.arange(SHEET_ENTRIES, dtype=jnp.int32)
    live = (owner[:, None] >= 0) & (
        page[:, None] * SHEET_ENTRIES + offsets[None, :] < slot_length[:, None]
    )
    stream = stream_in.astype(jnp.float32)
    qkv_cols = qkv_weight.shape[2]
    for layer_id in range(DEPTH_NUMBER):
        squares = jnp.sum(stream * stream, axis=1)
        scaled = (stream * attention_gain[layer_id][None, :]).astype(jnp.bfloat16)
        qkv_part = jnp.dot(scaled, qkv_weight[layer_id], preferred_element_type=jnp.float32)
        forget_part = jnp.dot(scaled, forget_weight[layer_id], preferred_element_type=jnp.float32)
        total = xor_sum(
            jnp.concatenate(
                [qkv_part.astype(jnp.bfloat16), forget_part.astype(jnp.bfloat16), split_pair(squares)],
                axis=1,
            ),
            "gx",
            jnp.float32,
        )
        rms_value = jnp.sqrt((total[:, -2] + total[:, -1]) / width + EPSILON)
        projected = (total[:, :qkv_cols] / rms_value[:, None]).reshape(
            request_count, local_heads, 3 * HEAD
        )
        forget_logit = total[:, qkv_cols : qkv_cols + local_heads] / rms_value[:, None]
        queries = projected[:, :, :HEAD].astype(jnp.bfloat16)
        new_keys = projected[:, :, HEAD : 2 * HEAD].astype(jnp.bfloat16)
        new_values = projected[:, :, 2 * HEAD :].astype(jnp.bfloat16)
        forget_log = jax.nn.log_sigmoid(forget_logit + forget_bias[layer_id][None, :])
        local_peak, local_sum, local_out = local_attention(
            queries, forget_log, layer_slice(kv_cache, layer_id), decay_cache[layer_id], owner, live, member
        )
        row_peak, row_sum, row_out = merge_pages(local_peak, local_sum, local_out)
        own_score = (
            jnp.sum(queries.astype(jnp.float32) * new_keys.astype(jnp.float32), axis=2)
            * SCORE_SCALE
        )
        full_peak = jnp.maximum(row_peak, own_score)
        cache_scale = jnp.exp(row_peak - full_peak)
        own_weight = jnp.exp(own_score - full_peak)
        own_rounded = lax.optimization_barrier(own_weight.astype(jnp.bfloat16)).astype(jnp.float32)
        numerator = cache_scale[:, :, None] * row_out + own_rounded[:, :, None] * new_values.astype(
            jnp.float32
        )
        denominator = cache_scale * row_sum + own_weight
        attended = (
            (numerator / denominator[:, :, None])
            .reshape(request_count, local_heads * HEAD)
            .astype(jnp.bfloat16)
        )
        stream = stream + core_first_sum(
            jnp.dot(attended, out_weight[layer_id], preferred_element_type=jnp.float32), "gy"
        )
        squares = jnp.sum(stream * stream, axis=1)
        scaled = (stream * feedforward_gain[layer_id][None, :]).astype(jnp.bfloat16)
        gate_part = jnp.dot(scaled, gate_weight[layer_id], preferred_element_type=jnp.float32)
        up_part = jnp.dot(scaled, up_weight[layer_id], preferred_element_type=jnp.float32)
        hidden_cols = gate_part.shape[1]
        total = gather_sum(
            jnp.concatenate(
                [gate_part.astype(jnp.bfloat16), up_part.astype(jnp.bfloat16), split_pair(squares)],
                axis=1,
            ),
            "gx",
        )
        rms_value = jnp.sqrt((total[:, -2] + total[:, -1]) / width + EPSILON)
        gate_full = total[:, :hidden_cols] / rms_value[:, None]
        up_full = total[:, hidden_cols : 2 * hidden_cols] / rms_value[:, None]
        hidden = (jax.nn.silu(gate_full) * up_full).astype(jnp.bfloat16)
        stream = stream + core_first_sum(
            jnp.dot(hidden, down_weight[layer_id], preferred_element_type=jnp.float32), "gy"
        )
    squares = jnp.sum(stream * stream, axis=1)
    scaled = (stream * final_gain[None, :]).astype(jnp.bfloat16)
    logits = jnp.dot(scaled, head_weight, preferred_element_type=jnp.float32)
    parts = lax.axis_size("gx")
    chunk = logits.shape[1] // parts
    squares_pair = split_pair(squares)
    pieces = jnp.concatenate(
        [
            logits.astype(jnp.bfloat16).reshape(request_count, parts, chunk),
            jnp.broadcast_to(squares_pair[:, None, :], (request_count, parts, 2)),
        ],
        axis=2,
    )
    pieces = lax.all_to_all(pieces, "gx", 1, 1, tiled=True).astype(jnp.float32)
    top_part = jnp.sum(pieces[:, :, :chunk], axis=1)
    total_squares = jnp.sum(pieces[:, :, chunk] + pieces[:, :, chunk + 1], axis=1)
    rms_value = jnp.sqrt(total_squares / width + EPSILON)
    final_hidden = (stream / rms_value[:, None] * final_gain[None, :]).astype(jnp.bfloat16)
    local_top = jnp.max(top_part, axis=1) / rms_value
    top_logits = core_first_max(xor_max(local_top, "gx"), "gy")
    return (final_hidden, rms_value, top_logits)


def solution(mesh):
    placed = (
        P(None, "gx"),
        P(None, "gx"),
        P(None, "gx"),
        P("gx"),
        P(None, "gx", "gy"),
        P(None, "gx", "gy"),
        P(None, "gy"),
        P(None, "gy", "gx"),
        P(None, "gx", "gy"),
        P(None, "gx", "gy"),
        P(None, "gy", "gx"),
        P("gx", "gy"),
        P(None, "gx", None, "gy", None),
        P(None, "gx", "gy", None),
        P(),
        P(),
    )
    return jax.shard_map(
        local, mesh=mesh, in_specs=placed, out_specs=(P(None, "gx"), P(), P()), check_vma=False
    )
```

```python
import jax
import jax.numpy as jnp
from jax import lax
from jax.sharding import PartitionSpec as P
from jax.experimental import pallas as pl
from jax.experimental.pallas import tpu as pltpu

HEAD = 64
DEPTH_NUMBER = 2
SHEET_ENTRIES = 128

SCORE_SCALE = 0.125
NEGATIVE = -1e30
EPSILON = 1e-06
LOW_BLOCK = 16


def gather_sum(value, axis):
    return jnp.sum(lax.all_gather(value, axis).astype(jnp.float32), axis=0)


def xor_sum(value, axis, kind=None):
    count = lax.axis_size(axis)
    parts = [value] + [
        lax.ppermute(value, axis, [(i, i ^ k) for i in range(count)]) for k in range(1, count)
    ]
    if kind is not None:
        parts = [part.astype(kind) for part in parts]
    while len(parts) > 1:
        parts = [parts[i] + parts[i + 1] for i in range(0, len(parts), 2)]
    return parts[0]


def butterfly(parts, join):
    while len(parts) > 1:
        parts = [join(parts[i], parts[i + 1]) for i in range(0, len(parts), 2)]
    return parts[0]


def exchange(value, axis, partner):
    count = lax.axis_size(axis)
    return lax.ppermute(value, axis, [(i, i ^ partner) for i in range(count)])


def core_first_sum(value, axis):
    carried = value.astype(jnp.bfloat16)
    pair = carried.astype(jnp.float32) + exchange(carried, axis, 1).astype(jnp.float32)
    pair = pair.astype(jnp.bfloat16)
    count = lax.axis_size(axis)
    parts = [pair] + [exchange(pair, axis, k) for k in range(2, count, 2)]
    return butterfly([part.astype(jnp.float32) for part in parts], jnp.add)


def core_first_max(value, axis):
    pair = jnp.maximum(value, exchange(value, axis, 1))
    count = lax.axis_size(axis)
    parts = [pair] + [exchange(pair, axis, k) for k in range(2, count, 2)]
    return butterfly(parts, jnp.maximum)


def split_pair(value):
    high = value.astype(jnp.bfloat16)
    low = (value - high.astype(jnp.float32)).astype(jnp.bfloat16)
    return jnp.stack([high, low], axis=1)


def xor_max(value, axis):
    count = lax.axis_size(axis)
    parts = [value] + [
        lax.ppermute(value, axis, [(i, i ^ k) for i in range(count)]) for k in range(1, count)
    ]
    while len(parts) > 1:
        parts = [jnp.maximum(parts[i], parts[i + 1]) for i in range(0, len(parts), 2)]
    return parts[0]


def copy_block(source, target):
    target[...] = source[...]


def layer_slice(cache, layer_id):
    layers, slots, tokens, heads, width = cache.shape
    block = 64
    return pl.pallas_call(
        copy_block,
        grid=(slots // block,),
        in_specs=[pl.BlockSpec((None, block, tokens, heads, width), lambda i: (layer_id, i, 0, 0, 0))],
        out_specs=pl.BlockSpec((block, tokens, heads, width), lambda i: (i, 0, 0, 0)),
        out_shape=jax.ShapeDtypeStruct((slots, tokens, heads, width), cache.dtype),
        cost_estimate=pl.CostEstimate(
            flops=0, transcendentals=0, bytes_accessed=2 * slots * tokens * heads * width * 2
        ),
    )(cache)


def local_slots(page_table, base, slot_count):
    request_count, page_count = page_table.shape
    flat = page_table.reshape(-1) - base
    valid = (flat >= 0) & (flat < slot_count)
    high = jnp.where(valid, flat // LOW_BLOCK, -1)
    low = flat % LOW_BLOCK
    entry = jnp.arange(request_count * page_count, dtype=jnp.int32)
    owner_code = (entry // page_count + 1).astype(jnp.float32)
    page_code = (entry % page_count).astype(jnp.float32)
    high_count = slot_count // LOW_BLOCK
    high_hot = (high[None, :] == jnp.arange(high_count, dtype=jnp.int32)[:, None]).astype(jnp.float32)
    low_hot = (low[None, :] == jnp.arange(LOW_BLOCK, dtype=jnp.int32)[:, None]).astype(jnp.bfloat16)
    coded = jnp.concatenate(
        [high_hot * owner_code[None, :], high_hot * page_code[None, :]], axis=0
    ).astype(jnp.bfloat16)
    table = lax.dot_general(
        coded, low_hot, (((1,), (1,)), ((), ())), preferred_element_type=jnp.float32
    )
    table = table.reshape(2, slot_count).astype(jnp.int32)
    owner = table[0] - 1
    page = table[1]
    return owner, page


def local_attention(queries, forget_log, kv_layer, decay_layer, owner, live, member):
    slots, tokens, heads, width = kv_layer.shape
    safe_owner = jnp.maximum(owner, 0)
    hot = member.T
    hot_half = hot.astype(jnp.bfloat16)
    hot_full = hot.astype(jnp.float32)
    slot_queries = jnp.einsum(
        "pr,rhd->phd", hot_half, queries, preferred_element_type=jnp.float32
    ).astype(jnp.bfloat16)
    padded = jnp.concatenate([slot_queries, jnp.zeros_like(slot_queries)], axis=2)
    diagonal = jnp.eye(heads, dtype=jnp.bfloat16)
    query_block = diagonal[None, :, :, None] * padded[:, :, None, :]
    scores = jnp.einsum(
        "pthc,pkhc->pkt", kv_layer, query_block, preferred_element_type=jnp.float32
    ) * SCORE_SCALE
    slot_forget = jnp.einsum("pr,rh->ph", hot_full, forget_log, precision=lax.Precision.HIGHEST)
    scores = scores + decay_layer + slot_forget[:, :, None]
    scores = jnp.where(live[:, None, :], scores, NEGATIVE)
    page_peak = jnp.max(scores, axis=2)
    row_peak = jnp.max(jnp.where(member[:, :, None], page_peak[None], NEGATIVE), axis=1)
    slot_peak = jnp.einsum("pr,rh->ph", hot_full, row_peak, precision=lax.Precision.HIGHEST)
    weights = jnp.where(live[:, None, :], jnp.exp(scores - slot_peak[:, :, None]), 0.0)
    page_sum = jnp.sum(weights, axis=2)
    weight_block = diagonal[None, :, None, :] * weights.astype(jnp.bfloat16)[:, :, :, None]
    mixed = jnp.einsum(
        "pkth,pthc->pkc", weight_block, kv_layer, preferred_element_type=jnp.float32
    )
    page_out = mixed[:, :, HEAD:]
    member_f = member.astype(jnp.float32)
    row_sum = jnp.einsum("rp,ph->rh", member_f, page_sum, precision=lax.Precision.HIGHEST)
    row_out = jnp.einsum("rp,phd->rhd", member_f, page_out, precision=lax.Precision.HIGHEST)
    return row_peak, row_sum, row_out


def merge_pages(row_peak, row_sum, row_out):
    packed = jnp.concatenate([row_peak[:, :, None], row_sum[:, :, None], row_out], axis=2)
    count = lax.axis_size("gx")
    every = [packed] + [exchange(packed, "gx", k) for k in range(1, count)]
    top = butterfly([part[:, :, 0] for part in every], jnp.maximum)
    scales = [jnp.exp(part[:, :, 0] - top) for part in every]
    total = butterfly([scale * part[:, :, 1] for scale, part in zip(scales, every)], jnp.add)
    out = butterfly(
        [scale[..., None] * part[:, :, 2:] for scale, part in zip(scales, every)], jnp.add
    )
    return top, total, out


def local(
    stream_in,
    attention_gain,
    feedforward_gain,
    final_gain,
    qkv_weight,
    forget_weight,
    forget_bias,
    out_weight,
    gate_weight,
    up_weight,
    down_weight,
    head_weight,
    kv_cache,
    decay_cache,
    lengths,
    page_table,
):
    local_pages = kv_cache.shape[1]
    local_heads = kv_cache.shape[3]
    request_count = stream_in.shape[0]
    width = stream_in.shape[1] * lax.axis_size("gx")
    base = lax.axis_index("gx") * local_pages
    owner, page = local_slots(page_table, base, local_pages)
    member = owner[None, :] == jnp.arange(request_count, dtype=jnp.int32)[:, None]
    slot_length = jnp.sum(jnp.where(member, lengths[:, None], 0), axis=0)
    offsets = jnp.arange(SHEET_ENTRIES, dtype=jnp.int32)
    live = (owner[:, None] >= 0) & (
        page[:, None] * SHEET_ENTRIES + offsets[None, :] < slot_length[:, None]
    )
    stream = stream_in.astype(jnp.float32)
    qkv_cols = qkv_weight.shape[2]
    for layer_id in range(DEPTH_NUMBER):
        squares = jnp.sum(stream * stream, axis=1)
        scaled = (stream * attention_gain[layer_id][None, :]).astype(jnp.bfloat16)
        qkv_part = jnp.dot(scaled, qkv_weight[layer_id], preferred_element_type=jnp.float32)
        forget_part = jnp.dot(scaled, forget_weight[layer_id], preferred_element_type=jnp.float32)
        total = xor_sum(
            jnp.concatenate(
                [qkv_part.astype(jnp.bfloat16), forget_part.astype(jnp.bfloat16), split_pair(squares)],
                axis=1,
            ),
            "gx",
            jnp.float32,
        )
        rms_value = jnp.sqrt((total[:, -2] + total[:, -1]) / width + EPSILON)
        projected = (total[:, :qkv_cols] / rms_value[:, None]).reshape(
            request_count, local_heads, 3 * HEAD
        )
        forget_logit = total[:, qkv_cols : qkv_cols + local_heads] / rms_value[:, None]
        queries = projected[:, :, :HEAD].astype(jnp.bfloat16)
        new_keys = projected[:, :, HEAD : 2 * HEAD].astype(jnp.bfloat16)
        new_values = projected[:, :, 2 * HEAD :].astype(jnp.bfloat16)
        forget_log = jax.nn.log_sigmoid(forget_logit + forget_bias[layer_id][None, :])
        local_peak, local_sum, local_out = local_attention(
            queries, forget_log, layer_slice(kv_cache, layer_id), decay_cache[layer_id], owner, live, member
        )
        row_peak, row_sum, row_out = merge_pages(local_peak, local_sum, local_out)
        own_score = (
            jnp.sum(queries.astype(jnp.float32) * new_keys.astype(jnp.float32), axis=2)
            * SCORE_SCALE
        )
        full_peak = jnp.maximum(row_peak, own_score)
        cache_scale = jnp.exp(row_peak - full_peak)
        own_weight = jnp.exp(own_score - full_peak)
        own_rounded = lax.optimization_barrier(own_weight.astype(jnp.bfloat16)).astype(jnp.float32)
        numerator = cache_scale[:, :, None] * row_out + own_rounded[:, :, None] * new_values.astype(
            jnp.float32
        )
        denominator = cache_scale * row_sum + own_weight
        attended = (
            (numerator / denominator[:, :, None])
            .reshape(request_count, local_heads * HEAD)
            .astype(jnp.bfloat16)
        )
        stream = stream + core_first_sum(
            jnp.dot(attended, out_weight[layer_id], preferred_element_type=jnp.float32), "gy"
        )
        squares = jnp.sum(stream * stream, axis=1)
        scaled = (stream * feedforward_gain[layer_id][None, :]).astype(jnp.bfloat16)
        gate_part = jnp.dot(scaled, gate_weight[layer_id], preferred_element_type=jnp.float32)
        up_part = jnp.dot(scaled, up_weight[layer_id], preferred_element_type=jnp.float32)
        hidden_cols = gate_part.shape[1]
        total = gather_sum(
            jnp.concatenate(
                [gate_part.astype(jnp.bfloat16), up_part.astype(jnp.bfloat16), split_pair(squares)],
                axis=1,
            ),
            "gx",
        )
        rms_value = jnp.sqrt((total[:, -2] + total[:, -1]) / width + EPSILON)
        gate_full = total[:, :hidden_cols] / rms_value[:, None]
        up_full = total[:, hidden_cols : 2 * hidden_cols] / rms_value[:, None]
        hidden = (jax.nn.silu(gate_full) * up_full).astype(jnp.bfloat16)
        stream = stream + core_first_sum(
            jnp.dot(hidden, down_weight[layer_id], preferred_element_type=jnp.float32), "gy"
        )
    squares = jnp.sum(stream * stream, axis=1)
    scaled = (stream * final_gain[None, :]).astype(jnp.bfloat16)
    logits = jnp.dot(scaled, head_weight, preferred_element_type=jnp.float32)
    parts = lax.axis_size("gx")
    chunk = logits.shape[1] // parts
    squares_pair = split_pair(squares)
    pieces = jnp.concatenate(
        [
            logits.astype(jnp.bfloat16).reshape(request_count, parts, chunk),
            jnp.broadcast_to(squares_pair[:, None, :], (request_count, parts, 2)),
        ],
        axis=2,
    )
    pieces = lax.all_to_all(pieces, "gx", 1, 1, tiled=True).astype(jnp.float32)
    top_part = jnp.sum(pieces[:, :, :chunk], axis=1)
    total_squares = jnp.sum(pieces[:, :, chunk] + pieces[:, :, chunk + 1], axis=1)
    rms_value = jnp.sqrt(total_squares / width + EPSILON)
    final_hidden = (stream / rms_value[:, None] * final_gain[None, :]).astype(jnp.bfloat16)
    local_top = jnp.max(top_part, axis=1) / rms_value
    top_logits = core_first_max(xor_max(local_top, "gx"), "gy")
    return (final_hidden, rms_value, top_logits)


def solution(mesh):
    placed = (
        P(None, "gx"),
        P(None, "gx"),
        P(None, "gx"),
        P("gx"),
        P(None, "gx", "gy"),
        P(None, "gx", "gy"),
        P(None, "gy"),
        P(None, "gy", "gx"),
        P(None, "gx", "gy"),
        P(None, "gx", "gy"),
        P(None, "gy", "gx"),
        P("gx", "gy"),
        P(None, "gx", None, "gy", None),
        P(None, "gx", "gy", None),
        P(),
        P(),
    )
    return jax.shard_map(
        local, mesh=mesh, in_specs=placed, out_specs=(P(None, "gx"), P(), P()), check_vma=False
    )
```

```python
import jax
import jax.numpy as jnp
from jax import lax
from jax.sharding import PartitionSpec as P
from jax.experimental import pallas as pl
from jax.experimental.pallas import tpu as pltpu

HEAD = 64
DEPTH_NUMBER = 2
SHEET_ENTRIES = 128

SCORE_SCALE = 0.125
NEGATIVE = -1e30
EPSILON = 1e-06
LOW_BLOCK = 16


def gather_sum(value, axis):
    return jnp.sum(lax.all_gather(value, axis).astype(jnp.float32), axis=0)


def xor_sum(value, axis, kind=None):
    count = lax.axis_size(axis)
    parts = [value] + [
        lax.ppermute(value, axis, [(i, i ^ k) for i in range(count)]) for k in range(1, count)
    ]
    if kind is not None:
        parts = [part.astype(kind) for part in parts]
    while len(parts) > 1:
        parts = [parts[i] + parts[i + 1] for i in range(0, len(parts), 2)]
    return parts[0]


def butterfly(parts, join):
    while len(parts) > 1:
        parts = [join(parts[i], parts[i + 1]) for i in range(0, len(parts), 2)]
    return parts[0]


def exchange(value, axis, partner):
    count = lax.axis_size(axis)
    return lax.ppermute(value, axis, [(i, i ^ partner) for i in range(count)])


def core_first_sum(value, axis):
    carried = value.astype(jnp.bfloat16)
    pair = carried.astype(jnp.float32) + exchange(carried, axis, 1).astype(jnp.float32)
    pair = pair.astype(jnp.bfloat16)
    count = lax.axis_size(axis)
    parts = [pair] + [exchange(pair, axis, k) for k in range(2, count, 2)]
    return butterfly([part.astype(jnp.float32) for part in parts], jnp.add)


def core_first_max(value, axis):
    pair = jnp.maximum(value, exchange(value, axis, 1))
    count = lax.axis_size(axis)
    parts = [pair] + [exchange(pair, axis, k) for k in range(2, count, 2)]
    return butterfly(parts, jnp.maximum)


def split_pair(value):
    high = value.astype(jnp.bfloat16)
    low = (value - high.astype(jnp.float32)).astype(jnp.bfloat16)
    return jnp.stack([high, low], axis=1)


def xor_max(value, axis):
    count = lax.axis_size(axis)
    parts = [value] + [
        lax.ppermute(value, axis, [(i, i ^ k) for i in range(count)]) for k in range(1, count)
    ]
    while len(parts) > 1:
        parts = [jnp.maximum(parts[i], parts[i + 1]) for i in range(0, len(parts), 2)]
    return parts[0]


def copy_block(source, target):
    target[...] = source[...]


def layer_slice(cache, layer_id):
    layers, slots, tokens, heads, width = cache.shape
    block = 64
    return pl.pallas_call(
        copy_block,
        grid=(slots // block,),
        in_specs=[pl.BlockSpec((None, block, tokens, heads, width), lambda i: (layer_id, i, 0, 0, 0))],
        out_specs=pl.BlockSpec((block, tokens, heads, width), lambda i: (i, 0, 0, 0)),
        out_shape=jax.ShapeDtypeStruct((slots, tokens, heads, width), cache.dtype),
        cost_estimate=pl.CostEstimate(
            flops=0, transcendentals=0, bytes_accessed=2 * slots * tokens * heads * width * 2
        ),
    )(cache)


def local_slots(page_table, base, slot_count):
    request_count, page_count = page_table.shape
    flat = page_table.reshape(-1) - base
    valid = (flat >= 0) & (flat < slot_count)
    high = jnp.where(valid, flat // LOW_BLOCK, -1)
    low = flat % LOW_BLOCK
    entry = jnp.arange(request_count * page_count, dtype=jnp.int32)
    owner_code = (entry // page_count + 1).astype(jnp.float32)
    page_code = (entry % page_count).astype(jnp.float32)
    high_count = slot_count // LOW_BLOCK
    high_hot = (high[None, :] == jnp.arange(high_count, dtype=jnp.int32)[:, None]).astype(jnp.float32)
    low_hot = (low[None, :] == jnp.arange(LOW_BLOCK, dtype=jnp.int32)[:, None]).astype(jnp.bfloat16)
    coded = jnp.concatenate(
        [high_hot * owner_code[None, :], high_hot * page_code[None, :]], axis=0
    ).astype(jnp.bfloat16)
    table = lax.dot_general(
        coded, low_hot, (((1,), (1,)), ((), ())), preferred_element_type=jnp.float32
    )
    table = table.reshape(2, slot_count).astype(jnp.int32)
    owner = table[0] - 1
    page = table[1]
    return owner, page


def local_attention(queries, forget_log, kv_layer, decay_layer, owner, live, member):
    slots, tokens, heads, width = kv_layer.shape
    safe_owner = jnp.maximum(owner, 0)
    hot = member.T
    hot_half = hot.astype(jnp.bfloat16)
    hot_full = hot.astype(jnp.float32)
    slot_queries = jnp.einsum(
        "pr,rhd->phd", hot_half, queries, preferred_element_type=jnp.float32
    ).astype(jnp.bfloat16)
    padded = jnp.concatenate([slot_queries, jnp.zeros_like(slot_queries)], axis=2)
    diagonal = jnp.eye(heads, dtype=jnp.bfloat16)
    query_block = diagonal[None, :, :, None] * padded[:, :, None, :]
    scores = jnp.einsum(
        "pthc,pkhc->pkt", kv_layer, query_block, preferred_element_type=jnp.float32
    ) * SCORE_SCALE
    slot_forget = jnp.einsum("pr,rh->ph", hot_full, forget_log, precision=lax.Precision.HIGHEST)
    scores = scores + decay_layer + slot_forget[:, :, None]
    scores = jnp.where(live[:, None, :], scores, NEGATIVE)
    page_peak = jnp.max(scores, axis=2)
    row_peak = jnp.max(jnp.where(member[:, :, None], page_peak[None], NEGATIVE), axis=1)
    slot_peak = jnp.einsum("pr,rh->ph", hot_full, row_peak, precision=lax.Precision.HIGHEST)
    weights = jnp.where(live[:, None, :], jnp.exp(scores - slot_peak[:, :, None]), 0.0)
    page_sum = jnp.sum(weights, axis=2)
    weight_block = diagonal[None, :, None, :] * weights.astype(jnp.bfloat16)[:, :, :, None]
    mixed = jnp.einsum(
        "pkth,pthc->pkc", weight_block, kv_layer, preferred_element_type=jnp.float32
    )
    page_out = mixed[:, :, HEAD:]
    member_f = member.astype(jnp.float32)
    packed = jnp.concatenate([page_sum[:, :, None], page_out], axis=2)
    row_all = jnp.einsum("rp,phd->rhd", member_f, packed, precision=lax.Precision.HIGHEST)
    return row_peak, row_all[:, :, 0], row_all[:, :, 1:]


def merge_pages(row_peak, row_sum, row_out):
    packed = jnp.concatenate([row_peak[:, :, None], row_sum[:, :, None], row_out], axis=2)
    count = lax.axis_size("gx")
    every = [packed] + [exchange(packed, "gx", k) for k in range(1, count)]
    top = butterfly([part[:, :, 0] for part in every], jnp.maximum)
    scales = [jnp.exp(part[:, :, 0] - top) for part in every]
    total = butterfly([scale * part[:, :, 1] for scale, part in zip(scales, every)], jnp.add)
    out = butterfly(
        [scale[..., None] * part[:, :, 2:] for scale, part in zip(scales, every)], jnp.add
    )
    return top, total, out


def local(
    stream_in,
    attention_gain,
    feedforward_gain,
    final_gain,
    qkv_weight,
    forget_weight,
    forget_bias,
    out_weight,
    gate_weight,
    up_weight,
    down_weight,
    head_weight,
    kv_cache,
    decay_cache,
    lengths,
    page_table,
):
    local_pages = kv_cache.shape[1]
    local_heads = kv_cache.shape[3]
    request_count = stream_in.shape[0]
    width = stream_in.shape[1] * lax.axis_size("gx")
    base = lax.axis_index("gx") * local_pages
    owner, page = local_slots(page_table, base, local_pages)
    member = owner[None, :] == jnp.arange(request_count, dtype=jnp.int32)[:, None]
    slot_length = jnp.sum(jnp.where(member, lengths[:, None], 0), axis=0)
    offsets = jnp.arange(SHEET_ENTRIES, dtype=jnp.int32)
    live = (owner[:, None] >= 0) & (
        page[:, None] * SHEET_ENTRIES + offsets[None, :] < slot_length[:, None]
    )
    stream = stream_in.astype(jnp.float32)
    qkv_cols = qkv_weight.shape[2]
    for layer_id in range(DEPTH_NUMBER):
        squares = jnp.sum(stream * stream, axis=1)
        scaled = (stream * attention_gain[layer_id][None, :]).astype(jnp.bfloat16)
        qkv_part = jnp.dot(scaled, qkv_weight[layer_id], preferred_element_type=jnp.float32)
        forget_part = jnp.dot(scaled, forget_weight[layer_id], preferred_element_type=jnp.float32)
        total = xor_sum(
            jnp.concatenate(
                [qkv_part.astype(jnp.bfloat16), forget_part.astype(jnp.bfloat16), split_pair(squares)],
                axis=1,
            ),
            "gx",
            jnp.float32,
        )
        rms_value = jnp.sqrt((total[:, -2] + total[:, -1]) / width + EPSILON)
        projected = (total[:, :qkv_cols] / rms_value[:, None]).reshape(
            request_count, local_heads, 3 * HEAD
        )
        forget_logit = total[:, qkv_cols : qkv_cols + local_heads] / rms_value[:, None]
        queries = projected[:, :, :HEAD].astype(jnp.bfloat16)
        new_keys = projected[:, :, HEAD : 2 * HEAD].astype(jnp.bfloat16)
        new_values = projected[:, :, 2 * HEAD :].astype(jnp.bfloat16)
        forget_log = jax.nn.log_sigmoid(forget_logit + forget_bias[layer_id][None, :])
        local_peak, local_sum, local_out = local_attention(
            queries, forget_log, layer_slice(kv_cache, layer_id), decay_cache[layer_id], owner, live, member
        )
        row_peak, row_sum, row_out = merge_pages(local_peak, local_sum, local_out)
        own_score = (
            jnp.sum(queries.astype(jnp.float32) * new_keys.astype(jnp.float32), axis=2)
            * SCORE_SCALE
        )
        full_peak = jnp.maximum(row_peak, own_score)
        cache_scale = jnp.exp(row_peak - full_peak)
        own_weight = jnp.exp(own_score - full_peak)
        own_rounded = lax.optimization_barrier(own_weight.astype(jnp.bfloat16)).astype(jnp.float32)
        numerator = cache_scale[:, :, None] * row_out + own_rounded[:, :, None] * new_values.astype(
            jnp.float32
        )
        denominator = cache_scale * row_sum + own_weight
        attended = (
            (numerator / denominator[:, :, None])
            .reshape(request_count, local_heads * HEAD)
            .astype(jnp.bfloat16)
        )
        stream = stream + core_first_sum(
            jnp.dot(attended, out_weight[layer_id], preferred_element_type=jnp.float32), "gy"
        )
        squares = jnp.sum(stream * stream, axis=1)
        scaled = (stream * feedforward_gain[layer_id][None, :]).astype(jnp.bfloat16)
        gate_part = jnp.dot(scaled, gate_weight[layer_id], preferred_element_type=jnp.float32)
        up_part = jnp.dot(scaled, up_weight[layer_id], preferred_element_type=jnp.float32)
        hidden_cols = gate_part.shape[1]
        total = gather_sum(
            jnp.concatenate(
                [gate_part.astype(jnp.bfloat16), up_part.astype(jnp.bfloat16), split_pair(squares)],
                axis=1,
            ),
            "gx",
        )
        rms_value = jnp.sqrt((total[:, -2] + total[:, -1]) / width + EPSILON)
        gate_full = total[:, :hidden_cols] / rms_value[:, None]
        up_full = total[:, hidden_cols : 2 * hidden_cols] / rms_value[:, None]
        hidden = (jax.nn.silu(gate_full) * up_full).astype(jnp.bfloat16)
        stream = stream + core_first_sum(
            jnp.dot(hidden, down_weight[layer_id], preferred_element_type=jnp.float32), "gy"
        )
    squares = jnp.sum(stream * stream, axis=1)
    scaled = (stream * final_gain[None, :]).astype(jnp.bfloat16)
    logits = jnp.dot(scaled, head_weight, preferred_element_type=jnp.float32)
    parts = lax.axis_size("gx")
    chunk = logits.shape[1] // parts
    squares_pair = split_pair(squares)
    pieces = jnp.concatenate(
        [
            logits.astype(jnp.bfloat16).reshape(request_count, parts, chunk),
            jnp.broadcast_to(squares_pair[:, None, :], (request_count, parts, 2)),
        ],
        axis=2,
    )
    pieces = lax.all_to_all(pieces, "gx", 1, 1, tiled=True).astype(jnp.float32)
    top_part = jnp.sum(pieces[:, :, :chunk], axis=1)
    total_squares = jnp.sum(pieces[:, :, chunk] + pieces[:, :, chunk + 1], axis=1)
    rms_value = jnp.sqrt(total_squares / width + EPSILON)
    final_hidden = (stream / rms_value[:, None] * final_gain[None, :]).astype(jnp.bfloat16)
    local_top = jnp.max(top_part, axis=1) / rms_value
    top_logits = core_first_max(xor_max(local_top, "gx"), "gy")
    return (final_hidden, rms_value, top_logits)


def solution(mesh):
    placed = (
        P(None, "gx"),
        P(None, "gx"),
        P(None, "gx"),
        P("gx"),
        P(None, "gx", "gy"),
        P(None, "gx", "gy"),
        P(None, "gy"),
        P(None, "gy", "gx"),
        P(None, "gx", "gy"),
        P(None, "gx", "gy"),
        P(None, "gy", "gx"),
        P("gx", "gy"),
        P(None, "gx", None, "gy", None),
        P(None, "gx", "gy", None),
        P(),
        P(),
    )
    return jax.shard_map(
        local, mesh=mesh, in_specs=placed, out_specs=(P(None, "gx"), P(), P()), check_vma=False
    )
```
